128 devices in a mesh: sta: 2 (over x_lo), gx: 16 (over x_hi, z, core), gy: 4 (over y).
Axes of the slice: x: 4 (x_hi: 2, x_lo: 2; x = x_hi * 2 + x_lo), y: 4, z: 4, core: 2. Of those that a mesh axis runs over, the one named last changes fastest.
Arguments:
- record: float32 [128, 1024], replicated, may hold values from -6 to 6
- shifts: int32 [128, 256], P(None, 'gx'), may hold values from 0 to 1022
- station_group: int32 [128], replicated, may hold values from 0 to 7
- weights: bfloat16 [128, 256, 512], P('sta', 'gy'), may hold values from -6 to 6
- psf_real: float32 [256, 256, 512], P(None, 'gx', 'gy'), may hold values from -6 to 6
- psf_imag: float32 [256, 256, 512], P(None, 'gx', 'gy'), may hold values from -6 to 6
Outputs:
- image: float32 [2, 256, 256, 512], P('sta', 'gx', 'gy')
The draws below stay inside these ranges and needn't reach their ends.
All inputs are finite; a program needn't handle non-finite values.
Results may differ from the reference program's by a relative error of at most 0.0029.
Values may be sent and summed in bfloat16 or wider, within the bound.
No kernel may reach another device: no remote copies, remote signals or barrier semaphores. Data moves between devices by JAX's collectives and lax.ppermute only.
A program may use at most 128 MiB of HBM per device.

```python
import math
import jax
import jax.numpy as jnp
import numpy as np
from jax import lax

STATIONS = 128
TIMES = 2
NZ = 256
NX = 256
NY = 512
TRACE = 1024
GROUPS = 8


def plant(array, stream_key, least, top_value):
    place = [jax.random.randint(jax.random.fold_in(stream_key, axis), (), 0, length) for axis, length in enumerate(array.shape)]
    widest = array.shape.index(max(array.shape))
    beside = place[:widest] + [(place[widest] + 1) % array.shape[widest]] + place[widest + 1:]
    return array.at[tuple(place)].set(least).at[tuple(beside)].set(top_value)


def block_levels(own_key, extent, split, smallest, high):
    factor_of = 1.0
    for position, blocks in split:
        heights = jax.random.uniform(jax.random.fold_in(jax.random.fold_in(own_key, 6), position), (blocks,), jnp.float32, smallest / len(split), high / len(split))
        factor_of = factor_of * jnp.repeat(jnp.exp(heights), extent[position] // blocks).reshape((-1,) + (1,) * (len(extent) - 1 - position))
    return factor_of


def cumulative_ranks(amount, lean):
    weights = [(1 << 20) // math.isqrt(standing ** lean) + 1 for standing in range(1, amount + 1)]
    spread = 1 + sum(weights) // (1 << 30)
    return np.cumsum(np.array([max(1, weight // spread) for weight in weights]))


def skewed_ids(stream_key, shape, number_of, skew):
    listing = cumulative_ranks(number_of, skew)
    lot = jax.random.randint(jax.random.fold_in(stream_key, 1), shape, 0, int(listing[number_of - 1]))
    rank = jnp.searchsorted(jnp.asarray(listing, jnp.int32), lot, side="right")
    return jax.random.permutation(jax.random.fold_in(stream_key, 2), number_of)[rank].astype(jnp.int32)


def centred(stream_key, extent, deviation, reach, shards=(), kind=jnp.bfloat16):
    factor_of = block_levels(stream_key, extent, shards, -0.22, 0.18) if shards else 1.0
    drawn = jax.random.normal(stream_key, extent, jnp.float32) * deviation * factor_of
    return jnp.minimum(jnp.maximum(drawn, -reach), reach).astype(kind)


def setup_inputs(seed: int = 0) -> dict:
    key_list = jax.random.split(jax.random.key(seed), 7)
    record = centred(key_list[0], (STATIONS, TRACE), 1.0, 6.0, (), jnp.float32)
    shifts = plant(jax.random.randint(key_list[1], (STATIONS, NZ), 0, TRACE - TIMES + 1), jax.random.fold_in(key_list[1], 1), 0, TRACE - TIMES).astype(jnp.int32)
    station_group = plant(skewed_ids(key_list[2], (STATIONS,), GROUPS, 2), jax.random.fold_in(key_list[2], 3), 0, GROUPS - 1).astype(jnp.int32)
    weights = centred(key_list[3], (STATIONS, NX, NY), 1.0, 6.0, ((0, 2), (1, 4)))
    psf_real = centred(key_list[4], (NZ, NX, NY), 1.0, 6.0, ((1, 16), (2, 4)), jnp.float32)
    psf_imag = centred(key_list[5], (NZ, NX, NY), 1.0, 6.0, ((1, 16), (2, 4)), jnp.float32)
    return dict(record=record, shifts=shifts, station_group=station_group, weights=weights, psf_real=psf_real, psf_imag=psf_imag)


NOISE_POWER = 0.25


def station_counts(station_group):
    labels = jnp.arange(GROUPS, dtype=jnp.int32)
    onehot = (station_group[:, None] == labels[None, :]).astype(jnp.float32)
    totals = jnp.sum(onehot, axis=0)
    return jnp.dot(onehot, totals, precision=lax.Precision.HIGHEST)


def coefficients(record, shifts, per_station, first_time, num_times):
    times_range = first_time + jnp.arange(num_times, dtype=jnp.int32)
    positions = (shifts[:, :, None] + times_range[None, None, :]).astype(jnp.int32)
    values = jnp.take_along_axis(record, positions.reshape(positions.shape[0], -1), axis=1)
    scaled = values.reshape(positions.shape) / per_station[:, None, None]
    return jnp.transpose(scaled, (2, 1, 0)).astype(jnp.bfloat16)


def reference(record, shifts, station_group, weights, psf_real, psf_imag):
    per_station = station_counts(station_group)
    coefficient = coefficients(record, shifts, per_station, 0, TIMES)
    stack = jnp.dot(coefficient.reshape(TIMES * NZ, STATIONS), weights.reshape(STATIONS, NX * NY),
                    preferred_element_type=jnp.float32).reshape(TIMES, NZ, NX, NY)
    spectrum = jnp.fft.fftn(stack, axes=(1, 2, 3))
    spec_real = jnp.real(spectrum)
    spec_imag = jnp.imag(spectrum)
    power = psf_real * psf_real + psf_imag * psf_imag + NOISE_POWER
    filt_real = (psf_real * spec_real + psf_imag * spec_imag) / power
    filt_imag = (psf_real * spec_imag - psf_imag * spec_real) / power
    result = jnp.fft.ifftn(filt_real + 1j * filt_imag, axes=(1, 2, 3))
    return jnp.real(result)
```

```python
import math

import jax
import jax.numpy as jnp
from jax import lax
from jax.sharding import PartitionSpec as P

TIMES = 2
GROUPS = 8
NOISE_POWER = 0.25
HIGHEST = lax.Precision.HIGHEST


def station_counts(station_group):
    labels = jnp.arange(GROUPS, dtype=jnp.int32)
    onehot = (station_group[:, None] == labels[None, :]).astype(jnp.float32)
    totals = jnp.sum(onehot, axis=0)
    return jnp.dot(onehot, totals, precision=HIGHEST)


def angles(rows, cols, length):
    product = rows[:, None] * cols[None, :] % length
    return product.astype(jnp.float32) * (2.0 * math.pi / length)


def local_coefficients(record, shifts, per_station):
    trace = record.shape[1]
    samples = jnp.arange(trace, dtype=jnp.int32)
    times = jnp.arange(TIMES, dtype=jnp.int32)
    positions = shifts[:, None, :] + times[None, :, None]
    hit = positions[:, :, :, None] == samples[None, None, None, :]
    values = jnp.sum(jnp.where(hit, record[:, None, None, :], 0.0), axis=3)
    scaled = values / per_station[:, None, None]
    return jnp.transpose(scaled, (1, 2, 0)).astype(jnp.bfloat16)


def on_device(record, shifts, station_group, weights, psf_real, psf_imag):
    n_sta = lax.axis_size("sta")
    n_gx = lax.axis_size("gx")
    n_gy = lax.axis_size("gy")
    k_sta = lax.axis_index("sta")
    per_station = station_counts(station_group)
    own = weights.shape[0]
    depth = shifts.shape[1]
    rows = weights.shape[1]
    width = weights.shape[2]
    nz = depth * n_gx
    nx = rows * n_gy
    cb = width // n_gy
    bb = nx // n_gx

    start = k_sta * own
    rec = lax.dynamic_slice_in_dim(record, start, own, 0)
    sh = lax.dynamic_slice_in_dim(shifts, start, own, 0)
    cnt = lax.dynamic_slice_in_dim(per_station, start, own, 0)
    coef = local_coefficients(rec, sh, cnt).reshape(TIMES * depth, own)
    partial = jnp.dot(
        coef, weights.reshape(own, rows * width), preferred_element_type=jnp.float32
    ).reshape(TIMES, depth, rows, width)
    send = lax.dynamic_index_in_dim(partial, 1 - k_sta, 0, keepdims=False)
    keep = lax.dynamic_index_in_dim(partial, k_sta, 0, keepdims=False)
    recv = lax.ppermute(send, "sta", [(i, (i + 1) % n_sta) for i in range(n_sta)])
    stack = keep + recv

    iy = jnp.arange(width, dtype=jnp.int32)
    ang_y = angles(iy, iy, width).reshape(width, n_gy, cb)
    ty = jnp.stack([jnp.cos(ang_y), -jnp.sin(ang_y)], axis=2)
    s1 = jnp.einsum("zxy,yjrc->jrzxc", stack, ty, precision=HIGHEST)
    s1 = lax.all_to_all(s1, "gy", 0, 0, tiled=True)
    s1 = s1.reshape(n_gy, 2, depth, rows, cb)

    ix = jnp.arange(nx, dtype=jnp.int32)
    ang_x = angles(ix, ix, nx)
    cx, sx = jnp.cos(ang_x), jnp.sin(ang_x)
    tx = jnp.stack([jnp.stack([cx, -sx], 1), jnp.stack([sx, cx], 1)], 0)
    tx = tx.reshape(2, n_gy, rows, 2, n_gx, bb)
    s2 = jnp.einsum("jszxc,sjxrib->irbzc", s1, tx, precision=HIGHEST)
    s2 = lax.all_to_all(s2, "gx", 0, 0, tiled=True)
    s2 = s2.reshape(n_gx, 2, bb, depth, cb)

    iz = jnp.arange(nz, dtype=jnp.int32)
    ang_z = angles(iz, iz, nz)
    cz, sz = jnp.cos(ang_z), jnp.sin(ang_z)
    tz = jnp.stack([jnp.stack([cz, -sz], 1), jnp.stack([sz, cz], 1)], 0)
    tz = tz.reshape(2, n_gx, depth, 2, nz)
    s3 = jnp.einsum("isbzc,sizra->rabc", s2, tz, precision=HIGHEST)

    power = psf_real * psf_real + psf_imag * psf_imag + NOISE_POWER
    f_re = (psf_real * s3[0] + psf_imag * s3[1]) / power
    f_im = (psf_real * s3[1] - psf_imag * s3[0]) / power
    filt = jnp.stack([f_re, f_im])

    scale_z = 1.0 / nz
    tzi = jnp.stack(
        [jnp.stack([cz, sz], 1), jnp.stack([-sz, cz], 1)], 0
    ) * scale_z
    tzi = tzi.reshape(2, nz, 2, n_gx, depth)
    g1 = jnp.einsum("sabc,sariz->irzbc", filt, tzi, precision=HIGHEST)
    g1 = lax.all_to_all(g1, "gx", 0, 0, tiled=True)
    g1 = g1.reshape(n_gx, 2, depth, bb, cb)

    scale_x = 1.0 / nx
    txi = jnp.stack(
        [jnp.stack([cx, sx], 1), jnp.stack([-sx, cx], 1)], 0
    ) * scale_x
    txi = txi.reshape(2, n_gx, bb, 2, n_gy, rows)
    g2 = jnp.einsum("iszbc,sibrjx->jrzxc", g1, txi, precision=HIGHEST)
    g2 = lax.all_to_all(g2, "gy", 0, 0, tiled=True)
    g2 = g2.reshape(n_gy, 2, depth, rows, cb)

    scale_y = 1.0 / width
    tyi = jnp.stack([jnp.cos(ang_y), -jnp.sin(ang_y)], axis=2) * scale_y
    image = jnp.einsum("jrzxc,yjrc->zxy", g2, tyi, precision=HIGHEST)
    return image[None]


def solution(mesh):
    in_specs = (
        P(),
        P(None, "gx"),
        P(),
        P("sta", "gy", None),
        P(None, "gx", "gy"),
        P(None, "gx", "gy"),
    )
    out_specs = P("sta", "gx", "gy", None)
    return jax.shard_map(
        on_device, mesh=mesh, in_specs=in_specs, out_specs=out_specs, check_vma=False
    )
```

```python
import math

import jax
import jax.numpy as jnp
from jax import lax
from jax.sharding import PartitionSpec as P

TIMES = 2
CHUNKS = 1
GROUPS = 8
NOISE_POWER = 0.25
HIGHEST = lax.Precision.HIGHEST
DFT = lax.Precision.HIGH


def station_counts(station_group):
    labels = jnp.arange(GROUPS, dtype=jnp.int32)
    onehot = (station_group[:, None] == labels[None, :]).astype(jnp.float32)
    totals = jnp.sum(onehot, axis=0)
    return jnp.dot(onehot, totals, precision=HIGHEST)


def angles(rows, cols, length):
    product = rows[:, None] * cols[None, :] % length
    return product.astype(jnp.float32) * (2.0 * math.pi / length)


def local_coefficients(record, shifts, per_station):
    trace = record.shape[1]
    samples = jnp.arange(trace, dtype=jnp.int32)
    times = jnp.arange(TIMES, dtype=jnp.int32)
    positions = shifts[:, None, :] + times[None, :, None]
    hit = positions[:, :, :, None] == samples[None, None, None, :]
    values = jnp.sum(jnp.where(hit, record[:, None, None, :], 0.0), axis=3)
    scaled = values / per_station[:, None, None]
    return jnp.transpose(scaled, (1, 2, 0)).astype(jnp.bfloat16)


def on_device(record, shifts, station_group, weights, psf_real, psf_imag):
    n_sta = lax.axis_size("sta")
    n_gx = lax.axis_size("gx")
    n_gy = lax.axis_size("gy")
    k_sta = lax.axis_index("sta")
    per_station = station_counts(station_group)
    own = weights.shape[0]
    depth = shifts.shape[1]
    rows = weights.shape[1]
    width = weights.shape[2]
    nz = depth * n_gx
    nx = rows * n_gy
    cb = width // n_gy
    bb = nx // n_gx

    start = k_sta * own
    rec = lax.dynamic_slice_in_dim(record, start, own, 0)
    sh = lax.dynamic_slice_in_dim(shifts, start, own, 0)
    cnt = lax.dynamic_slice_in_dim(per_station, start, own, 0)
    coef = local_coefficients(rec, sh, cnt).reshape(TIMES * depth, own)
    partial = jnp.dot(
        coef, weights.reshape(own, rows * width), preferred_element_type=jnp.float32
    ).reshape(TIMES, depth, rows, width)
    keep = lax.dynamic_index_in_dim(partial, k_sta, 0, keepdims=False)
    send = lax.dynamic_index_in_dim(partial, 1 - k_sta, 0, keepdims=False)
    pairs = [(i, (i + 1) % n_sta) for i in range(n_sta)]
    zc = depth // CHUNKS

    iy = jnp.arange(width, dtype=jnp.int32)
    ang_y = angles(iy, iy, width).reshape(width, n_gy, cb)
    ty = jnp.stack([jnp.cos(ang_y), -jnp.sin(ang_y)], axis=2)
    ix = jnp.arange(nx, dtype=jnp.int32)
    ang_x = angles(ix, ix, nx)
    cx, sx = jnp.cos(ang_x), jnp.sin(ang_x)
    tx = jnp.stack([jnp.stack([cx, -sx], 1), jnp.stack([sx, cx], 1)], 0)
    tx = tx.reshape(2, n_gy, rows, 2, n_gx, bb)
    iz = jnp.arange(nz, dtype=jnp.int32)
    ang_z = angles(iz, iz, nz)
    cz, sz = jnp.cos(ang_z), jnp.sin(ang_z)
    tz = jnp.stack([jnp.stack([cz, -sz], 1), jnp.stack([sz, cz], 1)], 0)
    tz = tz.reshape(2, n_gx, depth, 2, nz)

    s3 = None
    for k in range(CHUNKS):
        rows_k = slice(k * zc, (k + 1) * zc)
        recv = lax.ppermute(send[rows_k].astype(jnp.bfloat16), "sta", pairs)
        stack = keep[rows_k] + recv.astype(jnp.float32)
        s1 = jnp.einsum("zxy,yjrc->jrzxc", stack, ty, precision=DFT)
        s1 = lax.all_to_all(s1, "gy", 0, 0, tiled=True)
        s2 = jnp.einsum("jszxc,sjxrib->irbzc", s1, tx, precision=DFT)
        s2 = lax.all_to_all(s2, "gx", 0, 0, tiled=True)
        part = jnp.einsum("isbzc,sizra->rabc", s2, tz[:, :, rows_k], precision=DFT)
        s3 = part if s3 is None else s3 + part

    power = psf_real * psf_real + psf_imag * psf_imag + NOISE_POWER
    f_re = (psf_real * s3[0] + psf_imag * s3[1]) / power
    f_im = (psf_real * s3[1] - psf_imag * s3[0]) / power
    filt = jnp.stack([f_re, f_im])

    tzi = jnp.stack([jnp.stack([cz, sz], 1), jnp.stack([-sz, cz], 1)], 0) * (1.0 / nz)
    tzi = tzi.reshape(2, nz, 2, n_gx, depth)
    txi = jnp.stack([jnp.stack([cx, sx], 1), jnp.stack([-sx, cx], 1)], 0) * (1.0 / nx)
    txi = txi.reshape(2, n_gx, bb, 2, n_gy, rows)
    tyi = ty * (1.0 / width)

    pieces = []
    for k in range(CHUNKS):
        rows_k = slice(k * zc, (k + 1) * zc)
        g1 = jnp.einsum("sabc,sariz->irzbc", filt, tzi[..., rows_k], precision=DFT)
        g1 = lax.all_to_all(g1, "gx", 0, 0, tiled=True)
        g2 = jnp.einsum("iszbc,sibrjx->jrzxc", g1, txi, precision=DFT)
        g2 = lax.all_to_all(g2, "gy", 0, 0, tiled=True)
        pieces.append(jnp.einsum("jrzxc,yjrc->zxy", g2, tyi, precision=DFT))
    image = jnp.concatenate(pieces, axis=0)
    return image[None]


def solution(mesh):
    in_specs = (
        P(),
        P(None, "gx"),
        P(),
        P("sta", "gy", None),
        P(None, "gx", "gy"),
        P(None, "gx", "gy"),
    )
    out_specs = P("sta", "gx", "gy", None)
    return jax.shard_map(
        on_device, mesh=mesh, in_specs=in_specs, out_specs=out_specs, check_vma=False
    )
```

```python
import math

import jax
import jax.numpy as jnp
from jax import lax
from jax.sharding import PartitionSpec as P

TIMES = 2
CHUNKS = 1
GROUPS = 8
NOISE_POWER = 0.25
HIGHEST = lax.Precision.HIGHEST
DFT = lax.Precision.HIGH


def station_counts(station_group):
    labels = jnp.arange(GROUPS, dtype=jnp.int32)
    onehot = (station_group[:, None] == labels[None, :]).astype(jnp.float32)
    totals = jnp.sum(onehot, axis=0)
    return jnp.dot(onehot, totals, precision=HIGHEST)


def angles(rows, cols, length):
    product = rows[:, None] * cols[None, :] % length
    return product.astype(jnp.float32) * (2.0 * math.pi / length)


def local_coefficients(record, shifts, per_station):
    trace = record.shape[1]
    samples = jnp.arange(trace, dtype=jnp.int32)
    times = jnp.arange(TIMES, dtype=jnp.int32)
    positions = shifts[:, None, :] + times[None, :, None]
    hit = positions[:, :, :, None] == samples[None, None, None, :]
    values = jnp.sum(jnp.where(hit, record[:, None, None, :], 0.0), axis=3)
    scaled = values / per_station[:, None, None]
    return jnp.transpose(scaled, (1, 2, 0)).astype(jnp.bfloat16)


def on_device(record, shifts, station_group, weights, psf_real, psf_imag):
    n_sta = lax.axis_size("sta")
    n_gx = lax.axis_size("gx")
    n_gy = lax.axis_size("gy")
    k_sta = lax.axis_index("sta")
    per_station = station_counts(station_group)
    own = weights.shape[0]
    depth = shifts.shape[1]
    rows = weights.shape[1]
    width = weights.shape[2]
    nz = depth * n_gx
    nx = rows * n_gy
    cb = width // n_gy
    bb = nx // n_gx

    start = k_sta * own
    rec = lax.dynamic_slice_in_dim(record, start, own, 0)
    sh = lax.dynamic_slice_in_dim(shifts, start, own, 0)
    cnt = lax.dynamic_slice_in_dim(per_station, start, own, 0)
    coef = local_coefficients(rec, sh, cnt).reshape(TIMES * depth, own)
    partial = jnp.dot(
        coef, weights.reshape(own, rows * width), preferred_element_type=jnp.float32
    ).reshape(TIMES, depth, rows, width)
    keep = lax.dynamic_index_in_dim(partial, k_sta, 0, keepdims=False)
    send = lax.dynamic_index_in_dim(partial, 1 - k_sta, 0, keepdims=False)
    pairs = [(i, (i + 1) % n_sta) for i in range(n_sta)]
    zc = depth // CHUNKS

    iy = jnp.arange(width, dtype=jnp.int32)
    ang_y = angles(iy, iy, width).reshape(width, n_gy, cb)
    ty = jnp.stack([jnp.cos(ang_y), -jnp.sin(ang_y)], axis=2)
    ix = jnp.arange(nx, dtype=jnp.int32)
    ang_x = angles(ix, ix, nx)
    cx, sx = jnp.cos(ang_x), jnp.sin(ang_x)
    tx = jnp.stack([jnp.stack([cx, -sx], 1), jnp.stack([sx, cx], 1)], 0)
    tx = tx.reshape(2, n_gy, rows, 2, n_gx, bb)
    iz = jnp.arange(nz, dtype=jnp.int32)
    ang_z = angles(iz, iz, nz)
    cz, sz = jnp.cos(ang_z), jnp.sin(ang_z)
    tz = jnp.stack([jnp.stack([cz, -sz], 1), jnp.stack([sz, cz], 1)], 0)
    tz = tz.reshape(2, n_gx, depth, 2, nz)

    s3 = None
    for k in range(CHUNKS):
        rows_k = slice(k * zc, (k + 1) * zc)
        recv = lax.ppermute(send[rows_k].astype(jnp.bfloat16), "sta", pairs)
        stack = keep[rows_k] + recv.astype(jnp.float32)
        s1 = jnp.einsum("zxy,yjrc->jrzxc", stack, ty, precision=DFT)
        s1 = lax.all_to_all(s1, "gy", 0, 0, tiled=True)
        s2 = jnp.einsum("jszxc,sjxrib->irbzc", s1, tx, precision=DFT)
        s2 = lax.all_to_all(s2, "gx", 0, 0, tiled=True)
        part = jnp.einsum("isbzc,sizra->rabc", s2, tz[:, :, rows_k], precision=DFT)
        s3 = part if s3 is None else s3 + part

    power = psf_real * psf_real + psf_imag * psf_imag + NOISE_POWER
    f_re = (psf_real * s3[0] + psf_imag * s3[1]) / power
    f_im = (psf_real * s3[1] - psf_imag * s3[0]) / power
    filt = jnp.stack([f_re, f_im])

    tzi = jnp.stack([jnp.stack([cz, sz], 1), jnp.stack([-sz, cz], 1)], 0) * (1.0 / nz)
    tzi = tzi.reshape(2, nz, 2, n_gx, depth)
    txi = jnp.stack([jnp.stack([cx, sx], 1), jnp.stack([-sx, cx], 1)], 0) * (1.0 / nx)
    txi = txi.reshape(2, n_gx, bb, 2, n_gy, rows)
    tyi = ty * (1.0 / width)

    pieces = []
    for k in range(CHUNKS):
        rows_k = slice(k * zc, (k + 1) * zc)
        g1 = jnp.einsum("sabc,sariz->irzbc", filt, tzi[..., rows_k], precision=DFT)
        g1 = lax.all_to_all(g1.astype(jnp.bfloat16), "gx", 0, 0, tiled=True)
        g1 = g1.astype(jnp.float32)
        g2 = jnp.einsum("iszbc,sibrjx->jrzxc", g1, txi, precision=DFT)
        g2 = lax.all_to_all(g2, "gy", 0, 0, tiled=True)
        pieces.append(jnp.einsum("jrzxc,yjrc->zxy", g2, tyi, precision=DFT))
    image = jnp.concatenate(pieces, axis=0)
    return image[None]


def solution(mesh):
    in_specs = (
        P(),
        P(None, "gx"),
        P(),
        P("sta", "gy", None),
        P(None, "gx", "gy"),
        P(None, "gx", "gy"),
    )
    out_specs = P("sta", "gx", "gy", None)
    return jax.shard_map(
        on_device, mesh=mesh, in_specs=in_specs, out_specs=out_specs, check_vma=False
    )
```

```python
import math

import jax
import jax.numpy as jnp
from jax import lax
from jax.sharding import PartitionSpec as P

TIMES = 2
CHUNKS = 1
LINK_INV_Z = None
GROUPS = 8
NOISE_POWER = 0.25
HIGHEST = lax.Precision.HIGHEST
DFT = lax.Precision.HIGH


def station_counts(station_group):
    labels = jnp.arange(GROUPS, dtype=jnp.int32)
    onehot = (station_group[:, None] == labels[None, :]).astype(jnp.float32)
    totals = jnp.sum(onehot, axis=0)
    return jnp.dot(onehot, totals, precision=HIGHEST)


def angles(rows, cols, length):
    product = rows[:, None] * cols[None, :] % length
    return product.astype(jnp.float32) * (2.0 * math.pi / length)


def local_coefficients(record, shifts, per_station):
    trace = record.shape[1]
    samples = jnp.arange(trace, dtype=jnp.int32)
    times = jnp.arange(TIMES, dtype=jnp.int32)
    positions = shifts[:, None, :] + times[None, :, None]
    hit = positions[:, :, :, None] == samples[None, None, None, :]
    values = jnp.sum(jnp.where(hit, record[:, None, None, :], 0.0), axis=3)
    scaled = values / per_station[:, None, None]
    return jnp.transpose(scaled, (1, 2, 0)).astype(jnp.bfloat16)


def exchange(pieces, axis, n, link=None):
    out = [pieces[0]]
    for d in range(1, n):
        piece = pieces[d] if link is None else pieces[d].astype(link)
        got = lax.ppermute(piece, axis, [(s, (s + d) % n) for s in range(n)])
        out.append(got if link is None else got.astype(pieces.dtype))
    return jnp.stack(out)


def block_index(me, n, size, sign):
    d = jnp.arange(n, dtype=jnp.int32)[:, None]
    t = jnp.arange(size, dtype=jnp.int32)[None, :]
    return (((me + sign * d) % n) * size + t).reshape(-1)


def complex_block(rows, cols, length, sign, scale):
    ang = angles(rows, cols, length)
    cos, sin = jnp.cos(ang) * scale, jnp.sin(ang) * scale
    if sign < 0:
        return jnp.stack([jnp.stack([cos, -sin], 1), jnp.stack([sin, cos], 1)], 0)
    return jnp.stack([jnp.stack([cos, sin], 1), jnp.stack([-sin, cos], 1)], 0)


def on_device(record, shifts, station_group, weights, psf_real, psf_imag):
    n_sta = lax.axis_size("sta")
    n_gx = lax.axis_size("gx")
    n_gy = lax.axis_size("gy")
    k_sta = lax.axis_index("sta")
    k_gx = lax.axis_index("gx")
    k_gy = lax.axis_index("gy")
    per_station = station_counts(station_group)
    own = weights.shape[0]
    depth = shifts.shape[1]
    rows = weights.shape[1]
    width = weights.shape[2]
    nz = depth * n_gx
    nx = rows * n_gy
    cb = width // n_gy
    bb = nx // n_gx

    start = k_sta * own
    rec = lax.dynamic_slice_in_dim(record, start, own, 0)
    sh = lax.dynamic_slice_in_dim(shifts, start, own, 0)
    cnt = lax.dynamic_slice_in_dim(per_station, start, own, 0)
    coef = local_coefficients(rec, sh, cnt).reshape(TIMES * depth, own)
    partial = jnp.dot(
        coef, weights.reshape(own, rows * width), preferred_element_type=jnp.float32
    ).reshape(TIMES, depth, rows, width)
    keep = lax.dynamic_index_in_dim(partial, k_sta, 0, keepdims=False)
    send = lax.dynamic_index_in_dim(partial, 1 - k_sta, 0, keepdims=False)
    pairs = [(i, (i + 1) % n_sta) for i in range(n_sta)]
    zc = depth // CHUNKS

    iy = jnp.arange(width, dtype=jnp.int32)
    iz = jnp.arange(nz, dtype=jnp.int32)
    ang_y = angles(iy, block_index(k_gy, n_gy, cb, 1), width).reshape(width, n_gy, cb)
    ty = jnp.stack([jnp.cos(ang_y), -jnp.sin(ang_y)], axis=2)
    tx = complex_block(
        block_index(k_gy, n_gy, rows, -1), block_index(k_gx, n_gx, bb, 1), nx, -1, 1.0
    ).reshape(2, n_gy, rows, 2, n_gx, bb)
    tz = complex_block(block_index(k_gx, n_gx, depth, -1), iz, nz, -1, 1.0)
    tz = tz.reshape(2, n_gx, depth, 2, nz)

    s3 = None
    for k in range(CHUNKS):
        rows_k = slice(k * zc, (k + 1) * zc)
        recv = lax.ppermute(send[rows_k].astype(jnp.bfloat16), "sta", pairs)
        stack = keep[rows_k] + recv.astype(jnp.float32)
        s1 = jnp.einsum("zxy,ydrc->drzxc", stack, ty, precision=DFT)
        s1 = exchange(s1, "gy", n_gy)
        s2 = jnp.einsum("jszxc,sjxrib->irbzc", s1, tx, precision=DFT)
        s2 = exchange(s2, "gx", n_gx)
        part = jnp.einsum("isbzc,sizra->rabc", s2, tz[:, :, rows_k], precision=DFT)
        s3 = part if s3 is None else s3 + part

    power = psf_real * psf_real + psf_imag * psf_imag + NOISE_POWER
    f_re = (psf_real * s3[0] + psf_imag * s3[1]) / power
    f_im = (psf_real * s3[1] - psf_imag * s3[0]) / power
    filt = jnp.stack([f_re, f_im])

    tzi = complex_block(iz, block_index(k_gx, n_gx, depth, 1), nz, 1, 1.0 / nz)
    tzi = tzi.reshape(2, nz, 2, n_gx, depth)
    txi = complex_block(
        block_index(k_gx, n_gx, bb, -1), block_index(k_gy, n_gy, rows, 1), nx, 1, 1.0 / nx
    ).reshape(2, n_gx, bb, 2, n_gy, rows)
    ang_yi = angles(block_index(k_gy, n_gy, cb, -1), iy, width).reshape(n_gy, cb, width)
    tyi = jnp.stack([jnp.cos(ang_yi), -jnp.sin(ang_yi)], axis=1) * (1.0 / width)

    pieces = []
    for k in range(CHUNKS):
        rows_k = slice(k * zc, (k + 1) * zc)
        g1 = jnp.einsum("sabc,sariz->irzbc", filt, tzi[..., rows_k], precision=DFT)
        g1 = exchange(g1, "gx", n_gx, LINK_INV_Z)
        g2 = jnp.einsum("iszbc,sibrjx->jrzxc", g1, txi, precision=DFT)
        g2 = exchange(g2, "gy", n_gy)
        pieces.append(jnp.einsum("jrzxc,jrcy->zxy", g2, tyi, precision=DFT))
    image = jnp.concatenate(pieces, axis=0) if CHUNKS > 1 else pieces[0]
    return image[None]


def solution(mesh):
    in_specs = (
        P(),
        P(None, "gx"),
        P(),
        P("sta", "gy", None),
        P(None, "gx", "gy"),
        P(None, "gx", "gy"),
    )
    out_specs = P("sta", "gx", "gy", None)
    return jax.shard_map(
        on_device, mesh=mesh, in_specs=in_specs, out_specs=out_specs, check_vma=False
    )
```

```python
import math

import jax
import jax.numpy as jnp
from jax import lax
from jax.sharding import PartitionSpec as P

TIMES = 2
CHUNKS = 1
GROUPS = 8
NOISE_POWER = 0.25
HIGHEST = lax.Precision.HIGHEST
DFT = lax.Precision.HIGH


def station_counts(station_group):
    labels = jnp.arange(GROUPS, dtype=jnp.int32)
    onehot = (station_group[:, None] == labels[None, :]).astype(jnp.float32)
    totals = jnp.sum(onehot, axis=0)
    return jnp.dot(onehot, totals, precision=HIGHEST)


def angles(rows, cols, length):
    product = rows[:, None] * cols[None, :] % length
    return product.astype(jnp.float32) * (2.0 * math.pi / length)


def local_coefficients(record, shifts, per_station):
    trace = record.shape[1]
    samples = jnp.arange(trace, dtype=jnp.int32)
    times = jnp.arange(TIMES, dtype=jnp.int32)
    positions = shifts[:, None, :] + times[None, :, None]
    hit = positions[:, :, :, None] == samples[None, None, None, :]
    values = jnp.sum(jnp.where(hit, record[:, None, None, :], 0.0), axis=3)
    scaled = values / per_station[:, None, None]
    return jnp.transpose(scaled, (1, 2, 0)).astype(jnp.bfloat16)


def on_device(record, shifts, station_group, weights, psf_real, psf_imag):
    n_sta = lax.axis_size("sta")
    n_gx = lax.axis_size("gx")
    n_gy = lax.axis_size("gy")
    k_sta = lax.axis_index("sta")
    per_station = station_counts(station_group)
    own = weights.shape[0]
    depth = shifts.shape[1]
    rows = weights.shape[1]
    width = weights.shape[2]
    nz = depth * n_gx
    nx = rows * n_gy
    cb = width // n_gy
    bb = nx // n_gx

    start = k_sta * own
    rec = lax.dynamic_slice_in_dim(record, start, own, 0)
    sh = lax.dynamic_slice_in_dim(shifts, start, own, 0)
    cnt = lax.dynamic_slice_in_dim(per_station, start, own, 0)
    coef = local_coefficients(rec, sh, cnt).reshape(TIMES * depth, own)
    partial = jnp.dot(
        coef, weights.reshape(own, rows * width), preferred_element_type=jnp.float32
    ).reshape(TIMES, depth, rows, width)
    keep = lax.dynamic_index_in_dim(partial, k_sta, 0, keepdims=False)
    send = lax.dynamic_index_in_dim(partial, 1 - k_sta, 0, keepdims=False)
    pairs = [(i, (i + 1) % n_sta) for i in range(n_sta)]
    zc = depth // CHUNKS

    iy = jnp.arange(width, dtype=jnp.int32)
    ang_y = angles(iy, iy, width).reshape(width, n_gy, cb)
    ty = jnp.stack([jnp.cos(ang_y), -jnp.sin(ang_y)], axis=2)
    ix = jnp.arange(nx, dtype=jnp.int32)
    ang_x = angles(ix, ix, nx)
    cx, sx = jnp.cos(ang_x), jnp.sin(ang_x)
    tx = jnp.stack([jnp.stack([cx, -sx], 1), jnp.stack([sx, cx], 1)], 0)
    tx = tx.reshape(2, n_gy, rows, 2, n_gx, bb)
    iz = jnp.arange(nz, dtype=jnp.int32)
    ang_z = angles(iz, iz, nz)
    cz, sz = jnp.cos(ang_z), jnp.sin(ang_z)
    tz = jnp.stack([jnp.stack([cz, -sz], 1), jnp.stack([sz, cz], 1)], 0)
    tz = tz.reshape(2, n_gx, depth, 2, nz)

    s3 = None
    for k in range(CHUNKS):
        rows_k = slice(k * zc, (k + 1) * zc)
        recv = lax.ppermute(send[rows_k], "sta", pairs)
        stack = keep[rows_k] + recv
        s1 = jnp.einsum("zxy,yjrc->jrzxc", stack, ty, precision=DFT)
        s1 = lax.all_to_all(s1, "gy", 0, 0, tiled=True)
        s2 = jnp.einsum("jszxc,sjxrib->irbzc", s1, tx, precision=DFT)
        s2 = lax.all_to_all(s2, "gx", 0, 0, tiled=True)
        part = jnp.einsum("isbzc,sizra->rabc", s2, tz[:, :, rows_k], precision=DFT)
        s3 = part if s3 is None else s3 + part

    power = psf_real * psf_real + psf_imag * psf_imag + NOISE_POWER
    f_re = (psf_real * s3[0] + psf_imag * s3[1]) / power
    f_im = (psf_real * s3[1] - psf_imag * s3[0]) / power
    filt = jnp.stack([f_re, f_im])

    tzi = jnp.stack([jnp.stack([cz, sz], 1), jnp.stack([-sz, cz], 1)], 0) * (1.0 / nz)
    tzi = tzi.reshape(2, nz, 2, n_gx, depth)
    txi = jnp.stack([jnp.stack([cx, sx], 1), jnp.stack([-sx, cx], 1)], 0) * (1.0 / nx)
    txi = txi.reshape(2, n_gx, bb, 2, n_gy, rows)
    tyi = ty * (1.0 / width)

    pieces = []
    for k in range(CHUNKS):
        rows_k = slice(k * zc, (k + 1) * zc)
        g1 = jnp.einsum("sabc,sariz->irzbc", filt, tzi[..., rows_k], precision=DFT)
        g1 = lax.all_to_all(g1.astype(jnp.bfloat16), "gx", 0, 0, tiled=True)
        g1 = g1.astype(jnp.float32)
        g2 = jnp.einsum("iszbc,sibrjx->jrzxc", g1, txi, precision=DFT)
        g2 = lax.all_to_all(g2, "gy", 0, 0, tiled=True)
        pieces.append(jnp.einsum("jrzxc,yjrc->zxy", g2, tyi, precision=DFT))
    image = jnp.concatenate(pieces, axis=0)
    return image[None]


def solution(mesh):
    in_specs = (
        P(),
        P(None, "gx"),
        P(),
        P("sta", "gy", None),
        P(None, "gx", "gy"),
        P(None, "gx", "gy"),
    )
    out_specs = P("sta", "gx", "gy", None)
    return jax.shard_map(
        on_device, mesh=mesh, in_specs=in_specs, out_specs=out_specs, check_vma=False
    )
```

```python
import math

import jax
import jax.numpy as jnp
from jax import lax
from jax.sharding import PartitionSpec as P

TIMES = 2
LINK_INV_Z = jnp.bfloat16
GROUPS = 8
NOISE_POWER = 0.25
HIGHEST = lax.Precision.HIGHEST
DFT = lax.Precision.HIGH


def station_counts(station_group):
    labels = jnp.arange(GROUPS, dtype=jnp.int32)
    onehot = (station_group[:, None] == labels[None, :]).astype(jnp.float32)
    totals = jnp.sum(onehot, axis=0)
    return jnp.dot(onehot, totals, precision=HIGHEST)


def angles(rows, cols, length):
    product = rows[:, None] * cols[None, :] % length
    return product.astype(jnp.float32) * (2.0 * math.pi / length)


def local_coefficients(record, shifts, per_station):
    trace = record.shape[1]
    samples = jnp.arange(trace, dtype=jnp.int32)
    times = jnp.arange(TIMES, dtype=jnp.int32)
    positions = shifts[:, None, :] + times[None, :, None]
    hit = positions[:, :, :, None] == samples[None, None, None, :]
    values = jnp.sum(jnp.where(hit, record[:, None, None, :], 0.0), axis=3)
    scaled = values / per_station[:, None, None]
    return jnp.transpose(scaled, (1, 2, 0)).astype(jnp.bfloat16)


def complex_block(rows, cols, length, sign, scale):
    ang = angles(rows, cols, length)
    cos, sin = jnp.cos(ang) * scale, jnp.sin(ang) * scale
    if sign < 0:
        return jnp.stack([jnp.stack([cos, -sin], 1), jnp.stack([sin, cos], 1)], 0)
    return jnp.stack([jnp.stack([cos, sin], 1), jnp.stack([-sin, cos], 1)], 0)


def mirrored_psf(psf_real, psf_imag, k_sta, n_gx, n_gy, half):
    ext = jnp.stack([psf_real, psf_imag])
    below_gx = [(i, (i - 1) % n_gx) for i in range(n_gx)]
    below_gy = [(j, (j - 1) % n_gy) for j in range(n_gy)]
    ext = jnp.concatenate([ext, lax.ppermute(ext[:, :, :1], "gx", below_gx)], axis=2)
    ext = jnp.concatenate([ext, lax.ppermute(ext[:, :, :, :1], "gy", below_gy)], axis=3)
    first = 1 + half * (1 - k_sta)
    window = lax.dynamic_slice_in_dim(ext, first, half, axis=2)
    n = n_gx * n_gy
    opposite = [(i * n_gy + j, (n_gx - 1 - i) * n_gy + (n_gy - 1 - j))
                for i in range(n_gx) for j in range(n_gy)]
    window = lax.ppermute(window, ("gx", "gy"), opposite)
    window = jnp.roll(jnp.flip(window, axis=1), 1, axis=1)
    window = jnp.flip(window, axis=2)
    return jnp.flip(window[:, :, :, 1:], axis=3)


def on_device(record, shifts, station_group, weights, psf_real, psf_imag):
    n_sta = lax.axis_size("sta")
    n_gx = lax.axis_size("gx")
    n_gy = lax.axis_size("gy")
    k_sta = lax.axis_index("sta")
    per_station = station_counts(station_group)
    own = weights.shape[0]
    depth = shifts.shape[1]
    rows = weights.shape[1]
    width = weights.shape[2]
    nz = depth * n_gx
    nx = rows * n_gy
    cb = width // n_gy
    bb = nx // n_gx
    zh = depth // n_sta
    bh = bb // n_sta
    n_grp = n_gx * n_sta
    pairs = [(i, (i + 1) % n_sta) for i in range(n_sta)]

    mirror = mirrored_psf(psf_real, psf_imag, k_sta, n_gx, n_gy, bh)

    start = k_sta * own
    rec = lax.dynamic_slice_in_dim(record, start, own, 0)
    sh = lax.dynamic_slice_in_dim(shifts, start, own, 0)
    cnt = lax.dynamic_slice_in_dim(per_station, start, own, 0)
    coef = local_coefficients(rec, sh, cnt).reshape(TIMES * depth, own)
    partial = jnp.dot(
        coef, weights.reshape(own, rows * width), preferred_element_type=jnp.float32
    ).reshape(TIMES, depth, rows, width)
    keep = lax.dynamic_slice_in_dim(partial, k_sta * zh, zh, axis=1)
    send = lax.dynamic_slice_in_dim(partial, (1 - k_sta) * zh, zh, axis=1)
    field = keep + lax.ppermute(send, "sta", pairs)

    iy = jnp.arange(width, dtype=jnp.int32)
    ix = jnp.arange(nx, dtype=jnp.int32)
    iz = jnp.arange(nz, dtype=jnp.int32)
    ty = complex_block(iy, iy, width, -1, 1.0).reshape(2, width, 2, n_gy, cb)
    s1 = jnp.einsum("szxy,syrjc->jrzxc", field, ty, precision=DFT)
    s1 = lax.all_to_all(s1, "gy", 0, 0, tiled=True)
    tx = complex_block(ix, ix, nx, -1, 1.0).reshape(2, n_gy, rows, 2, n_grp, bh)
    s2 = jnp.einsum("jszxc,sjxrLb->Lrbzc", s1, tx, precision=DFT)
    s2 = lax.all_to_all(s2, ("gx", "sta"), 0, 0, tiled=True)
    tz = complex_block(iz, iz, nz, -1, 1.0).reshape(2, n_grp, zh, 2, nz)
    s3 = jnp.einsum("Lsbzc,sLzra->rabc", s2, tz, precision=DFT)

    pr = lax.dynamic_slice_in_dim(psf_real, k_sta * bh, bh, axis=1)
    pi = lax.dynamic_slice_in_dim(psf_imag, k_sta * bh, bh, axis=1)
    pw = pr * pr + pi * pi + NOISE_POWER
    mr, mi = mirror[0], mirror[1]
    mw = mr * mr + mi * mi + NOISE_POWER
    we_re = 0.5 * (pr / pw + mr / mw)
    we_im = 0.5 * (mi / mw - pi / pw)
    h_re = we_re * s3[0] - we_im * s3[1]
    h_im = we_re * s3[1] + we_im * s3[0]
    filt = jnp.stack([h_re, h_im])

    tzi = complex_block(iz, iz, nz, 1, 1.0 / nz).reshape(2, nz, 2, n_grp, zh)
    g1 = jnp.einsum("sabc,sarLz->Lrzbc", filt, tzi, precision=DFT)
    if LINK_INV_Z is not None:
        g1 = g1.astype(LINK_INV_Z)
    g1 = lax.all_to_all(g1, ("gx", "sta"), 0, 0, tiled=True).astype(jnp.float32)
    txi = complex_block(ix, ix, nx, 1, 1.0 / nx).reshape(2, n_grp, bh, 2, n_gy, rows)
    g2 = jnp.einsum("Lszbc,sLbrjx->jrzxc", g1, txi, precision=DFT)
    g2 = lax.all_to_all(g2, "gy", 0, 0, tiled=True)
    tyi = complex_block(iy, iy, width, 1, 1.0 / width).reshape(2, n_gy, cb, 2, width)
    both = jnp.einsum("jszxc,sjcry->rzxy", g2, tyi, precision=DFT)

    mine = lax.dynamic_index_in_dim(both, k_sta, 0, keepdims=False)
    other = lax.ppermute(lax.dynamic_index_in_dim(both, 1 - k_sta, 0, keepdims=False), "sta", pairs)
    first = jnp.where(k_sta == 0, mine, other)
    second = jnp.where(k_sta == 0, other, mine)
    return jnp.concatenate([first, second], axis=0)[None]


def solution(mesh):
    in_specs = (
        P(),
        P(None, "gx"),
        P(),
        P("sta", "gy", None),
        P(None, "gx", "gy"),
        P(None, "gx", "gy"),
    )
    out_specs = P("sta", "gx", "gy", None)
    return jax.shard_map(
        on_device, mesh=mesh, in_specs=in_specs, out_specs=out_specs, check_vma=False
    )
```

```python
import math

import jax
import jax.numpy as jnp
from jax import lax
from jax.sharding import PartitionSpec as P

TIMES = 2
LINK_INV_Z = jnp.bfloat16
GROUPS = 8
NOISE_POWER = 0.25
HIGHEST = lax.Precision.HIGHEST
DFT = lax.Precision.HIGH


def station_counts(station_group):
    labels = jnp.arange(GROUPS, dtype=jnp.int32)
    onehot = (station_group[:, None] == labels[None, :]).astype(jnp.float32)
    totals = jnp.sum(onehot, axis=0)
    return jnp.dot(onehot, totals, precision=HIGHEST)


def angles(rows, cols, length):
    product = rows[:, None] * cols[None, :] % length
    return product.astype(jnp.float32) * (2.0 * math.pi / length)


def local_coefficients(record, shifts, per_station):
    trace = record.shape[1]
    samples = jnp.arange(trace, dtype=jnp.int32)
    times = jnp.arange(TIMES, dtype=jnp.int32)
    positions = shifts[:, None, :] + times[None, :, None]
    hit = positions[:, :, :, None] == samples[None, None, None, :]
    values = jnp.sum(jnp.where(hit, record[:, None, None, :], 0.0), axis=3)
    scaled = values / per_station[:, None, None]
    return jnp.transpose(scaled, (1, 2, 0)).astype(jnp.bfloat16)


def complex_block(rows, cols, length, sign, scale):
    ang = angles(rows, cols, length)
    cos, sin = jnp.cos(ang) * scale, jnp.sin(ang) * scale
    if sign < 0:
        return jnp.stack([jnp.stack([cos, -sin], 1), jnp.stack([sin, cos], 1)], 0)
    return jnp.stack([jnp.stack([cos, sin], 1), jnp.stack([-sin, cos], 1)], 0)


def mirrored_psf(psf_real, psf_imag, k_sta, n_gx, n_gy, half, barrier=None):
    both = jnp.stack([psf_real, psf_imag])
    nz, bb, cb = both.shape[1], both.shape[2], both.shape[3]
    n = n_gx * n_gy

    def send(piece, di, dj):
        pairs = [(i * n_gy + j, ((di - i) % n_gx) * n_gy + (dj - j) % n_gy)
                 for i in range(n_gx) for j in range(n_gy)]
        return lax.ppermute(piece, ("gx", "gy"), pairs)

    rows = lax.dynamic_slice_in_dim(both, half - (half - 1) * k_sta, half, axis=2)
    main = send(rows, n_gx - 1, n_gy - 1)
    col = send(rows[:, :, :, :1], n_gx - 1, n_gy)
    row = send(both[:, :, :1], n_gx, n_gy - 1)
    corner = send(both[:, :, :1, :1], n_gx, n_gy)
    window = jnp.concatenate(
        [jnp.concatenate([main, col], axis=3), jnp.concatenate([row, corner], axis=3)], axis=2
    )
    ia = jnp.arange(nz, dtype=jnp.int32)
    flip_a = (ia[:, None] == (nz - ia[None, :]) % nz).astype(jnp.float32)
    it = jnp.arange(half + 1, dtype=jnp.int32)[:, None]
    tb = jnp.arange(half, dtype=jnp.int32)[None, :]
    flip_t = (it == half - 1 - tb + 1 - k_sta).astype(jnp.float32)
    iu = jnp.arange(cb + 1, dtype=jnp.int32)[:, None]
    uc = jnp.arange(cb, dtype=jnp.int32)[None, :]
    flip_u = (iu == cb - uc).astype(jnp.float32)
    window = lax.optimization_barrier(window) if barrier is None else lax.optimization_barrier((window, barrier))
    window, barrier = window if isinstance(window, tuple) else (window, None)
    out = jnp.einsum("rxyz,zc->rxyc", window, flip_u, precision=HIGHEST)
    out = jnp.einsum("rxyc,yb->rxbc", out, flip_t, precision=HIGHEST)
    return jnp.einsum("rxbc,xa->rabc", out, flip_a, precision=HIGHEST), barrier


def on_device(record, shifts, station_group, weights, psf_real, psf_imag):
    n_sta = lax.axis_size("sta")
    n_gx = lax.axis_size("gx")
    n_gy = lax.axis_size("gy")
    k_sta = lax.axis_index("sta")
    per_station = station_counts(station_group)
    own = weights.shape[0]
    depth = shifts.shape[1]
    rows = weights.shape[1]
    width = weights.shape[2]
    nz = depth * n_gx
    nx = rows * n_gy
    cb = width // n_gy
    bb = nx // n_gx
    zh = depth // n_sta
    bh = bb // n_sta
    n_grp = n_gx * n_sta
    pairs = [(i, (i + 1) % n_sta) for i in range(n_sta)]

    start = k_sta * own
    rec = lax.dynamic_slice_in_dim(record, start, own, 0)
    sh = lax.dynamic_slice_in_dim(shifts, start, own, 0)
    cnt = lax.dynamic_slice_in_dim(per_station, start, own, 0)
    coef = local_coefficients(rec, sh, cnt).reshape(TIMES * depth, own)
    partial = jnp.dot(
        coef, weights.reshape(own, rows * width), preferred_element_type=jnp.float32
    ).reshape(TIMES, depth, rows, width)
    keep = lax.dynamic_slice_in_dim(partial, k_sta * zh, zh, axis=1)
    send = lax.dynamic_slice_in_dim(partial, (1 - k_sta) * zh, zh, axis=1)
    field = keep + lax.ppermute(send, "sta", pairs)
    mirror, field = mirrored_psf(psf_real, psf_imag, k_sta, n_gx, n_gy, bh, field)

    iy = jnp.arange(width, dtype=jnp.int32)
    ix = jnp.arange(nx, dtype=jnp.int32)
    iz = jnp.arange(nz, dtype=jnp.int32)
    ty = complex_block(iy, iy, width, -1, 1.0).reshape(2, width, 2, n_gy, cb)
    s1 = jnp.einsum("szxy,syrjc->jrzxc", field, ty, precision=DFT)
    s1 = lax.all_to_all(s1, "gy", 0, 0, tiled=True)
    tx = complex_block(ix, ix, nx, -1, 1.0).reshape(2, n_gy, rows, 2, n_grp, bh)
    s2 = jnp.einsum("jszxc,sjxrLb->Lrbzc", s1, tx, precision=DFT)
    s2 = lax.all_to_all(s2, ("gx", "sta"), 0, 0, tiled=True)
    tz = complex_block(iz, iz, nz, -1, 1.0).reshape(2, n_grp, zh, 2, nz)
    s3 = jnp.einsum("Lsbzc,sLzra->rabc", s2, tz, precision=DFT)

    pr = lax.dynamic_slice_in_dim(psf_real, k_sta * bh, bh, axis=1)
    pi = lax.dynamic_slice_in_dim(psf_imag, k_sta * bh, bh, axis=1)
    pw = pr * pr + pi * pi + NOISE_POWER
    mr, mi = mirror[0], mirror[1]
    mw = mr * mr + mi * mi + NOISE_POWER
    we_re = 0.5 * (pr / pw + mr / mw)
    we_im = 0.5 * (mi / mw - pi / pw)
    h_re = we_re * s3[0] - we_im * s3[1]
    h_im = we_re * s3[1] + we_im * s3[0]
    filt = jnp.stack([h_re, h_im])

    tzi = complex_block(iz, iz, nz, 1, 1.0 / nz).reshape(2, nz, 2, n_grp, zh)
    g1 = jnp.einsum("sabc,sarLz->Lrzbc", filt, tzi, precision=DFT)
    if LINK_INV_Z is not None:
        g1 = g1.astype(LINK_INV_Z)
    g1 = lax.all_to_all(g1, ("gx", "sta"), 0, 0, tiled=True).astype(jnp.float32)
    txi = complex_block(ix, ix, nx, 1, 1.0 / nx).reshape(2, n_grp, bh, 2, n_gy, rows)
    g2 = jnp.einsum("Lszbc,sLbrjx->jrzxc", g1, txi, precision=DFT)
    g2 = lax.all_to_all(g2, "gy", 0, 0, tiled=True)
    tyi = complex_block(iy, iy, width, 1, 1.0 / width).reshape(2, n_gy, cb, 2, width)
    both = jnp.einsum("jszxc,sjcry->rzxy", g2, tyi, precision=DFT)

    mine = lax.dynamic_index_in_dim(both, k_sta, 0, keepdims=False)
    other = lax.ppermute(lax.dynamic_index_in_dim(both, 1 - k_sta, 0, keepdims=False), "sta", pairs)
    first = jnp.where(k_sta == 0, mine, other)
    second = jnp.where(k_sta == 0, other, mine)
    return jnp.concatenate([first, second], axis=0)[None]


def solution(mesh):
    in_specs = (
        P(),
        P(None, "gx"),
        P(),
        P("sta", "gy", None),
        P(None, "gx", "gy"),
        P(None, "gx", "gy"),
    )
    out_specs = P("sta", "gx", "gy", None)
    return jax.shard_map(
        on_device, mesh=mesh, in_specs=in_specs, out_specs=out_specs, check_vma=False
    )
```

```python
import math

import jax
import jax.numpy as jnp
from jax import lax
from jax.sharding import PartitionSpec as P

TIMES = 2
LINK_INV_Z = jnp.bfloat16
GROUPS = 8
NOISE_POWER = 0.25
HIGHEST = lax.Precision.HIGHEST
DFT = lax.Precision.HIGH


def station_counts(station_group):
    labels = jnp.arange(GROUPS, dtype=jnp.int32)
    onehot = (station_group[:, None] == labels[None, :]).astype(jnp.float32)
    totals = jnp.sum(onehot, axis=0)
    return jnp.dot(onehot, totals, precision=HIGHEST)


def angles(rows, cols, length):
    product = rows[:, None] * cols[None, :] % length
    return product.astype(jnp.float32) * (2.0 * math.pi / length)


def local_coefficients(record, shifts, per_station):
    trace = record.shape[1]
    samples = jnp.arange(trace, dtype=jnp.int32)
    times = jnp.arange(TIMES, dtype=jnp.int32)
    positions = shifts[:, None, :] + times[None, :, None]
    hit = positions[:, :, :, None] == samples[None, None, None, :]
    values = jnp.sum(jnp.where(hit, record[:, None, None, :], 0.0), axis=3)
    scaled = values / per_station[:, None, None]
    return jnp.transpose(scaled, (1, 2, 0)).astype(jnp.bfloat16)


def complex_block(rows, cols, length, sign, scale):
    ang = angles(rows, cols, length)
    cos, sin = jnp.cos(ang) * scale, jnp.sin(ang) * scale
    if sign < 0:
        return jnp.stack([jnp.stack([cos, -sin], 1), jnp.stack([sin, cos], 1)], 0)
    return jnp.stack([jnp.stack([cos, sin], 1), jnp.stack([-sin, cos], 1)], 0)


def mirrored_psf(psf_real, psf_imag, k_sta, n_gx, n_gy, half, barrier=None):
    both = jnp.stack([psf_real, psf_imag])
    nz, bb, cb = both.shape[1], both.shape[2], both.shape[3]
    n = n_gx * n_gy

    def send(piece, di, dj):
        pairs = [(q * n + i * n_gy + j, (1 - q) * n + ((di - i) % n_gx) * n_gy + (dj - j) % n_gy)
                 for q in range(2) for i in range(n_gx) for j in range(n_gy)]
        return lax.ppermute(piece, ("sta", "gx", "gy"), pairs)

    rows = lax.dynamic_slice_in_dim(both, half - (half - 1) * (1 - k_sta), half, axis=2)
    main = send(rows, n_gx - 1, n_gy - 1)
    col = send(rows[:, :, :, :1], n_gx - 1, n_gy)
    row = send(both[:, :, :1], n_gx, n_gy - 1)
    corner = send(both[:, :, :1, :1], n_gx, n_gy)
    window = jnp.concatenate(
        [jnp.concatenate([main, col], axis=3), jnp.concatenate([row, corner], axis=3)], axis=2
    )
    ia = jnp.arange(nz, dtype=jnp.int32)
    flip_a = (ia[:, None] == (nz - ia[None, :]) % nz).astype(jnp.float32)
    it = jnp.arange(half + 1, dtype=jnp.int32)[:, None]
    tb = jnp.arange(half, dtype=jnp.int32)[None, :]
    flip_t = (it == half - 1 - tb + 1 - k_sta).astype(jnp.float32)
    iu = jnp.arange(cb + 1, dtype=jnp.int32)[:, None]
    uc = jnp.arange(cb, dtype=jnp.int32)[None, :]
    flip_u = (iu == cb - uc).astype(jnp.float32)
    window = lax.optimization_barrier(window) if barrier is None else lax.optimization_barrier((window, barrier))
    window, barrier = window if isinstance(window, tuple) else (window, None)
    out = jnp.einsum("rxyz,zc->rxyc", window, flip_u, precision=HIGHEST)
    out = jnp.einsum("rxyc,yb->rxbc", out, flip_t, precision=HIGHEST)
    return jnp.einsum("rxbc,xa->rabc", out, flip_a, precision=HIGHEST), barrier


def on_device(record, shifts, station_group, weights, psf_real, psf_imag):
    n_sta = lax.axis_size("sta")
    n_gx = lax.axis_size("gx")
    n_gy = lax.axis_size("gy")
    k_sta = lax.axis_index("sta")
    per_station = station_counts(station_group)
    own = weights.shape[0]
    depth = shifts.shape[1]
    rows = weights.shape[1]
    width = weights.shape[2]
    nz = depth * n_gx
    nx = rows * n_gy
    cb = width // n_gy
    bb = nx // n_gx
    zh = depth // n_sta
    bh = bb // n_sta
    n_grp = n_gx * n_sta
    pairs = [(i, (i + 1) % n_sta) for i in range(n_sta)]

    start = k_sta * own
    rec = lax.dynamic_slice_in_dim(record, start, own, 0)
    sh = lax.dynamic_slice_in_dim(shifts, start, own, 0)
    cnt = lax.dynamic_slice_in_dim(per_station, start, own, 0)
    coef = local_coefficients(rec, sh, cnt).reshape(TIMES * depth, own)
    partial = jnp.dot(
        coef, weights.reshape(own, rows * width), preferred_element_type=jnp.float32
    ).reshape(TIMES, depth, rows, width)
    keep = lax.dynamic_slice_in_dim(partial, k_sta * zh, zh, axis=1)
    send = lax.dynamic_slice_in_dim(partial, (1 - k_sta) * zh, zh, axis=1)
    field = keep + lax.ppermute(send, "sta", pairs)
    mirror, field = mirrored_psf(psf_real, psf_imag, k_sta, n_gx, n_gy, bh, field)

    iy = jnp.arange(width, dtype=jnp.int32)
    ix = jnp.arange(nx, dtype=jnp.int32)
    iz = jnp.arange(nz, dtype=jnp.int32)
    ty = complex_block(iy, iy, width, -1, 1.0).reshape(2, width, 2, n_gy, cb)
    s1 = jnp.einsum("szxy,syrjc->jrzxc", field, ty, precision=DFT)
    s1 = lax.all_to_all(s1, "gy", 0, 0, tiled=True)
    tx = complex_block(ix, ix, nx, -1, 1.0).reshape(2, n_gy, rows, 2, n_grp, bh)
    s2 = jnp.einsum("jszxc,sjxrLb->Lrbzc", s1, tx, precision=DFT)
    s2 = lax.all_to_all(s2, ("gx", "sta"), 0, 0, tiled=True)
    tz = complex_block(iz, iz, nz, -1, 1.0).reshape(2, n_grp, zh, 2, nz)
    s3 = jnp.einsum("Lsbzc,sLzra->rabc", s2, tz, precision=DFT)

    pr = lax.dynamic_slice_in_dim(psf_real, k_sta * bh, bh, axis=1)
    pi = lax.dynamic_slice_in_dim(psf_imag, k_sta * bh, bh, axis=1)
    pw = pr * pr + pi * pi + NOISE_POWER
    mr, mi = mirror[0], mirror[1]
    mw = mr * mr + mi * mi + NOISE_POWER
    we_re = 0.5 * (pr / pw + mr / mw)
    we_im = 0.5 * (mi / mw - pi / pw)
    h_re = we_re * s3[0] - we_im * s3[1]
    h_im = we_re * s3[1] + we_im * s3[0]
    filt = jnp.stack([h_re, h_im])

    tzi = complex_block(iz, iz, nz, 1, 1.0 / nz).reshape(2, nz, 2, n_grp, zh)
    g1 = jnp.einsum("sabc,sarLz->Lrzbc", filt, tzi, precision=DFT)
    if LINK_INV_Z is not None:
        g1 = g1.astype(LINK_INV_Z)
    g1 = lax.all_to_all(g1, ("gx", "sta"), 0, 0, tiled=True).astype(jnp.float32)
    txi = complex_block(ix, ix, nx, 1, 1.0 / nx).reshape(2, n_grp, bh, 2, n_gy, rows)
    g2 = jnp.einsum("Lszbc,sLbrjx->jrzxc", g1, txi, precision=DFT)
    g2 = lax.all_to_all(g2, "gy", 0, 0, tiled=True)
    tyi = complex_block(iy, iy, width, 1, 1.0 / width).reshape(2, n_gy, cb, 2, width)
    both = jnp.einsum("jszxc,sjcry->rzxy", g2, tyi, precision=DFT)

    mine = lax.dynamic_index_in_dim(both, k_sta, 0, keepdims=False)
    other = lax.ppermute(lax.dynamic_index_in_dim(both, 1 - k_sta, 0, keepdims=False), "sta", pairs)
    first = jnp.where(k_sta == 0, mine, other)
    second = jnp.where(k_sta == 0, other, mine)
    return jnp.concatenate([first, second], axis=0)[None]


def solution(mesh):
    in_specs = (
        P(),
        P(None, "gx"),
        P(),
        P("sta", "gy", None),
        P(None, "gx", "gy"),
        P(None, "gx", "gy"),
    )
    out_specs = P("sta", "gx", "gy", None)
    return jax.shard_map(
        on_device, mesh=mesh, in_specs=in_specs, out_specs=out_specs, check_vma=False
    )
```

```python
import math

import jax
import jax.numpy as jnp
from jax import lax
from jax.sharding import PartitionSpec as P

TIMES = 2
LINK_INV_Z = None
LINK_STA = jnp.bfloat16
GROUPS = 8
NOISE_POWER = 0.25
HIGHEST = lax.Precision.HIGHEST
DFT = lax.Precision.HIGH


def station_counts(station_group):
    labels = jnp.arange(GROUPS, dtype=jnp.int32)
    onehot = (station_group[:, None] == labels[None, :]).astype(jnp.float32)
    totals = jnp.sum(onehot, axis=0)
    return jnp.dot(onehot, totals, precision=HIGHEST)


def angles(rows, cols, length):
    product = rows[:, None] * cols[None, :] % length
    return product.astype(jnp.float32) * (2.0 * math.pi / length)


def local_coefficients(record, shifts, per_station):
    trace = record.shape[1]
    samples = jnp.arange(trace, dtype=jnp.int32)
    times = jnp.arange(TIMES, dtype=jnp.int32)
    positions = shifts[:, None, :] + times[None, :, None]
    hit = positions[:, :, :, None] == samples[None, None, None, :]
    values = jnp.sum(jnp.where(hit, record[:, None, None, :], 0.0), axis=3)
    scaled = values / per_station[:, None, None]
    return jnp.transpose(scaled, (1, 2, 0)).astype(jnp.bfloat16)


def complex_block(rows, cols, length, sign, scale):
    ang = angles(rows, cols, length)
    cos, sin = jnp.cos(ang) * scale, jnp.sin(ang) * scale
    if sign < 0:
        return jnp.stack([jnp.stack([cos, -sin], 1), jnp.stack([sin, cos], 1)], 0)
    return jnp.stack([jnp.stack([cos, sin], 1), jnp.stack([-sin, cos], 1)], 0)


def mirrored_psf(psf_real, psf_imag, k_sta, n_gx, n_gy, half, barrier=None):
    both = jnp.stack([psf_real, psf_imag])
    nz, bb, cb = both.shape[1], both.shape[2], both.shape[3]
    n = n_gx * n_gy

    def send(piece, di, dj):
        pairs = [(q * n + i * n_gy + j, (1 - q) * n + ((di - i) % n_gx) * n_gy + (dj - j) % n_gy)
                 for q in range(2) for i in range(n_gx) for j in range(n_gy)]
        return lax.ppermute(piece, ("sta", "gx", "gy"), pairs)

    rows = lax.dynamic_slice_in_dim(both, half - (half - 1) * (1 - k_sta), half, axis=2)
    main = send(rows, n_gx - 1, n_gy - 1)
    col = send(rows[:, :, :, :1], n_gx - 1, n_gy)
    row = send(both[:, :, :1], n_gx, n_gy - 1)
    corner = send(both[:, :, :1, :1], n_gx, n_gy)
    window = jnp.concatenate(
        [jnp.concatenate([main, col], axis=3), jnp.concatenate([row, corner], axis=3)], axis=2
    )
    ia = jnp.arange(nz, dtype=jnp.int32)
    flip_a = (ia[:, None] == (nz - ia[None, :]) % nz).astype(jnp.float32)
    it = jnp.arange(half + 1, dtype=jnp.int32)[:, None]
    tb = jnp.arange(half, dtype=jnp.int32)[None, :]
    flip_t = (it == half - 1 - tb + 1 - k_sta).astype(jnp.float32)
    iu = jnp.arange(cb + 1, dtype=jnp.int32)[:, None]
    uc = jnp.arange(cb, dtype=jnp.int32)[None, :]
    flip_u = (iu == cb - uc).astype(jnp.float32)
    window = lax.optimization_barrier(window) if barrier is None else lax.optimization_barrier((window, barrier))
    window, barrier = window if isinstance(window, tuple) else (window, None)
    out = jnp.einsum("rxyz,zc->rxyc", window, flip_u, precision=HIGHEST)
    out = jnp.einsum("rxyc,yb->rxbc", out, flip_t, precision=HIGHEST)
    return jnp.einsum("rxbc,xa->rabc", out, flip_a, precision=HIGHEST), barrier


def on_device(record, shifts, station_group, weights, psf_real, psf_imag):
    n_sta = lax.axis_size("sta")
    n_gx = lax.axis_size("gx")
    n_gy = lax.axis_size("gy")
    k_sta = lax.axis_index("sta")
    per_station = station_counts(station_group)
    own = weights.shape[0]
    depth = shifts.shape[1]
    rows = weights.shape[1]
    width = weights.shape[2]
    nz = depth * n_gx
    nx = rows * n_gy
    cb = width // n_gy
    bb = nx // n_gx
    zh = depth // n_sta
    bh = bb // n_sta
    n_grp = n_gx * n_sta
    pairs = [(i, (i + 1) % n_sta) for i in range(n_sta)]

    start = k_sta * own
    rec = lax.dynamic_slice_in_dim(record, start, own, 0)
    sh = lax.dynamic_slice_in_dim(shifts, start, own, 0)
    cnt = lax.dynamic_slice_in_dim(per_station, start, own, 0)
    coef = local_coefficients(rec, sh, cnt).reshape(TIMES * depth, own)
    partial = jnp.dot(
        coef, weights.reshape(own, rows * width), preferred_element_type=jnp.float32
    ).reshape(TIMES, depth, rows, width)
    keep = lax.dynamic_slice_in_dim(partial, k_sta * zh, zh, axis=1)
    send = lax.dynamic_slice_in_dim(partial, (1 - k_sta) * zh, zh, axis=1)
    field = keep + lax.ppermute(send.astype(LINK_STA), "sta", pairs).astype(jnp.float32)
    mirror, field = mirrored_psf(psf_real, psf_imag, k_sta, n_gx, n_gy, bh, field)

    iy = jnp.arange(width, dtype=jnp.int32)
    ix = jnp.arange(nx, dtype=jnp.int32)
    iz = jnp.arange(nz, dtype=jnp.int32)
    ty = complex_block(iy, iy, width, -1, 1.0).reshape(2, width, 2, n_gy, cb)
    s1 = jnp.einsum("szxy,syrjc->jrzxc", field, ty, precision=DFT)
    s1 = lax.all_to_all(s1, "gy", 0, 0, tiled=True)
    tx = complex_block(ix, ix, nx, -1, 1.0).reshape(2, n_gy, rows, 2, n_grp, bh)
    s2 = jnp.einsum("jszxc,sjxrLb->Lrbzc", s1, tx, precision=DFT)
    s2 = lax.all_to_all(s2, ("gx", "sta"), 0, 0, tiled=True)
    tz = complex_block(iz, iz, nz, -1, 1.0).reshape(2, n_grp, zh, 2, nz)
    s3 = jnp.einsum("Lsbzc,sLzra->rabc", s2, tz, precision=DFT)

    pr = lax.dynamic_slice_in_dim(psf_real, k_sta * bh, bh, axis=1)
    pi = lax.dynamic_slice_in_dim(psf_imag, k_sta * bh, bh, axis=1)
    pw = pr * pr + pi * pi + NOISE_POWER
    mr, mi = mirror[0], mirror[1]
    mw = mr * mr + mi * mi + NOISE_POWER
    we_re = 0.5 * (pr / pw + mr / mw)
    we_im = 0.5 * (mi / mw - pi / pw)
    h_re = we_re * s3[0] - we_im * s3[1]
    h_im = we_re * s3[1] + we_im * s3[0]
    filt = jnp.stack([h_re, h_im])

    tzi = complex_block(iz, iz, nz, 1, 1.0 / nz).reshape(2, nz, 2, n_grp, zh)
    g1 = jnp.einsum("sabc,sarLz->Lrzbc", filt, tzi, precision=DFT)
    if LINK_INV_Z is not None:
        g1 = g1.astype(LINK_INV_Z)
    g1 = lax.all_to_all(g1, ("gx", "sta"), 0, 0, tiled=True).astype(jnp.float32)
    txi = complex_block(ix, ix, nx, 1, 1.0 / nx).reshape(2, n_grp, bh, 2, n_gy, rows)
    g2 = jnp.einsum("Lszbc,sLbrjx->jrzxc", g1, txi, precision=DFT)
    g2 = lax.all_to_all(g2, "gy", 0, 0, tiled=True)
    tyi = complex_block(iy, iy, width, 1, 1.0 / width).reshape(2, n_gy, cb, 2, width)
    both = jnp.einsum("jszxc,sjcry->rzxy", g2, tyi, precision=DFT)

    mine = lax.dynamic_index_in_dim(both, k_sta, 0, keepdims=False)
    other = lax.ppermute(lax.dynamic_index_in_dim(both, 1 - k_sta, 0, keepdims=False), "sta", pairs)
    first = jnp.where(k_sta == 0, mine, other)
    second = jnp.where(k_sta == 0, other, mine)
    return jnp.concatenate([first, second], axis=0)[None]


def solution(mesh):
    in_specs = (
        P(),
        P(None, "gx"),
        P(),
        P("sta", "gy", None),
        P(None, "gx", "gy"),
        P(None, "gx", "gy"),
    )
    out_specs = P("sta", "gx", "gy", None)
    return jax.shard_map(
        on_device, mesh=mesh, in_specs=in_specs, out_specs=out_specs, check_vma=False
    )
```

```python
import math

import jax
import jax.numpy as jnp
from jax import lax
from jax.sharding import PartitionSpec as P

TIMES = 2
LINK_INV_Z = jnp.bfloat16
TAIL_CHUNKS = 2
GROUPS = 8
NOISE_POWER = 0.25
HIGHEST = lax.Precision.HIGHEST
DFT = lax.Precision.HIGH


def station_counts(station_group):
    labels = jnp.arange(GROUPS, dtype=jnp.int32)
    onehot = (station_group[:, None] == labels[None, :]).astype(jnp.float32)
    totals = jnp.sum(onehot, axis=0)
    return jnp.dot(onehot, totals, precision=HIGHEST)


def angles(rows, cols, length):
    product = rows[:, None] * cols[None, :] % length
    return product.astype(jnp.float32) * (2.0 * math.pi / length)


def local_coefficients(record, shifts, per_station):
    trace = record.shape[1]
    samples = jnp.arange(trace, dtype=jnp.int32)
    times = jnp.arange(TIMES, dtype=jnp.int32)
    positions = shifts[:, None, :] + times[None, :, None]
    hit = positions[:, :, :, None] == samples[None, None, None, :]
    values = jnp.sum(jnp.where(hit, record[:, None, None, :], 0.0), axis=3)
    scaled = values / per_station[:, None, None]
    return jnp.transpose(scaled, (1, 2, 0)).astype(jnp.bfloat16)


def complex_block(rows, cols, length, sign, scale):
    ang = angles(rows, cols, length)
    cos, sin = jnp.cos(ang) * scale, jnp.sin(ang) * scale
    if sign < 0:
        return jnp.stack([jnp.stack([cos, -sin], 1), jnp.stack([sin, cos], 1)], 0)
    return jnp.stack([jnp.stack([cos, sin], 1), jnp.stack([-sin, cos], 1)], 0)


def mirrored_psf(psf_real, psf_imag, k_sta, n_gx, n_gy, half, barrier=None):
    both = jnp.stack([psf_real, psf_imag])
    nz, bb, cb = both.shape[1], both.shape[2], both.shape[3]
    n = n_gx * n_gy

    def send(piece, di, dj):
        pairs = [(q * n + i * n_gy + j, (1 - q) * n + ((di - i) % n_gx) * n_gy + (dj - j) % n_gy)
                 for q in range(2) for i in range(n_gx) for j in range(n_gy)]
        return lax.ppermute(piece, ("sta", "gx", "gy"), pairs)

    rows = lax.dynamic_slice_in_dim(both, half - (half - 1) * (1 - k_sta), half, axis=2)
    main = send(rows, n_gx - 1, n_gy - 1)
    col = send(rows[:, :, :, :1], n_gx - 1, n_gy)
    row = send(both[:, :, :1], n_gx, n_gy - 1)
    corner = send(both[:, :, :1, :1], n_gx, n_gy)
    window = jnp.concatenate(
        [jnp.concatenate([main, col], axis=3), jnp.concatenate([row, corner], axis=3)], axis=2
    )
    ia = jnp.arange(nz, dtype=jnp.int32)
    flip_a = (ia[:, None] == (nz - ia[None, :]) % nz).astype(jnp.float32)
    it = jnp.arange(half + 1, dtype=jnp.int32)[:, None]
    tb = jnp.arange(half, dtype=jnp.int32)[None, :]
    flip_t = (it == half - 1 - tb + 1 - k_sta).astype(jnp.float32)
    iu = jnp.arange(cb + 1, dtype=jnp.int32)[:, None]
    uc = jnp.arange(cb, dtype=jnp.int32)[None, :]
    flip_u = (iu == cb - uc).astype(jnp.float32)
    window = lax.optimization_barrier(window) if barrier is None else lax.optimization_barrier((window, barrier))
    window, barrier = window if isinstance(window, tuple) else (window, None)
    out = jnp.einsum("rxyz,zc->rxyc", window, flip_u, precision=HIGHEST)
    out = jnp.einsum("rxyc,yb->rxbc", out, flip_t, precision=HIGHEST)
    return jnp.einsum("rxbc,xa->rabc", out, flip_a, precision=HIGHEST), barrier


def on_device(record, shifts, station_group, weights, psf_real, psf_imag):
    n_sta = lax.axis_size("sta")
    n_gx = lax.axis_size("gx")
    n_gy = lax.axis_size("gy")
    k_sta = lax.axis_index("sta")
    per_station = station_counts(station_group)
    own = weights.shape[0]
    depth = shifts.shape[1]
    rows = weights.shape[1]
    width = weights.shape[2]
    nz = depth * n_gx
    nx = rows * n_gy
    cb = width // n_gy
    bb = nx // n_gx
    zh = depth // n_sta
    bh = bb // n_sta
    n_grp = n_gx * n_sta
    pairs = [(i, (i + 1) % n_sta) for i in range(n_sta)]

    start = k_sta * own
    rec = lax.dynamic_slice_in_dim(record, start, own, 0)
    sh = lax.dynamic_slice_in_dim(shifts, start, own, 0)
    cnt = lax.dynamic_slice_in_dim(per_station, start, own, 0)
    coef = local_coefficients(rec, sh, cnt).reshape(TIMES * depth, own)
    partial = jnp.dot(
        coef, weights.reshape(own, rows * width), preferred_element_type=jnp.float32
    ).reshape(TIMES, depth, rows, width)
    keep = lax.dynamic_slice_in_dim(partial, k_sta * zh, zh, axis=1)
    send = lax.dynamic_slice_in_dim(partial, (1 - k_sta) * zh, zh, axis=1)
    field = keep + lax.ppermute(send, "sta", pairs)
    mirror, field = mirrored_psf(psf_real, psf_imag, k_sta, n_gx, n_gy, bh, field)

    iy = jnp.arange(width, dtype=jnp.int32)
    ix = jnp.arange(nx, dtype=jnp.int32)
    iz = jnp.arange(nz, dtype=jnp.int32)
    ty = complex_block(iy, iy, width, -1, 1.0).reshape(2, width, 2, n_gy, cb)
    s1 = jnp.einsum("szxy,syrjc->jrzxc", field, ty, precision=DFT)
    s1 = lax.all_to_all(s1, "gy", 0, 0, tiled=True)
    tx = complex_block(ix, ix, nx, -1, 1.0).reshape(2, n_gy, rows, 2, n_grp, bh)
    s2 = jnp.einsum("jszxc,sjxrLb->Lrbzc", s1, tx, precision=DFT)
    s2 = lax.all_to_all(s2, ("gx", "sta"), 0, 0, tiled=True)
    tz = complex_block(iz, iz, nz, -1, 1.0).reshape(2, n_grp, zh, 2, nz)
    s3 = jnp.einsum("Lsbzc,sLzra->rabc", s2, tz, precision=DFT)

    pr = lax.dynamic_slice_in_dim(psf_real, k_sta * bh, bh, axis=1)
    pi = lax.dynamic_slice_in_dim(psf_imag, k_sta * bh, bh, axis=1)
    pw = pr * pr + pi * pi + NOISE_POWER
    mr, mi = mirror[0], mirror[1]
    mw = mr * mr + mi * mi + NOISE_POWER
    we_re = 0.5 * (pr / pw + mr / mw)
    we_im = 0.5 * (mi / mw - pi / pw)
    h_re = we_re * s3[0] - we_im * s3[1]
    h_im = we_re * s3[1] + we_im * s3[0]
    filt = jnp.stack([h_re, h_im])

    tzi = complex_block(iz, iz, nz, 1, 1.0 / nz).reshape(2, nz, 2, n_grp, zh)
    g1 = jnp.einsum("sabc,sarLz->Lrzbc", filt, tzi, precision=DFT)
    if LINK_INV_Z is not None:
        g1 = g1.astype(LINK_INV_Z)
    g1 = lax.all_to_all(g1, ("gx", "sta"), 0, 0, tiled=True).astype(jnp.float32)
    txi = complex_block(ix, ix, nx, 1, 1.0 / nx).reshape(2, n_grp, bh, 2, n_gy, rows)
    tyi = complex_block(iy, iy, width, 1, 1.0 / width).reshape(2, n_gy, cb, 2, width)
    zt = zh // TAIL_CHUNKS
    mines, others = [], []
    for k in range(TAIL_CHUNKS):
        g2 = jnp.einsum("Lszbc,sLbrjx->jrzxc", g1[:, :, k * zt:(k + 1) * zt], txi, precision=DFT)
        g2 = lax.all_to_all(g2, "gy", 0, 0, tiled=True)
        both = jnp.einsum("jszxc,sjcry->rzxy", g2, tyi, precision=DFT)
        mines.append(lax.dynamic_index_in_dim(both, k_sta, 0, keepdims=False))
        others.append(lax.ppermute(
            lax.dynamic_index_in_dim(both, 1 - k_sta, 0, keepdims=False), "sta", pairs))
    mine = jnp.concatenate(mines, axis=0)
    other = jnp.concatenate(others, axis=0)
    first = jnp.where(k_sta == 0, mine, other)
    second = jnp.where(k_sta == 0, other, mine)
    return jnp.concatenate([first, second], axis=0)[None]


def solution(mesh):
    in_specs = (
        P(),
        P(None, "gx"),
        P(),
        P("sta", "gy", None),
        P(None, "gx", "gy"),
        P(None, "gx", "gy"),
    )
    out_specs = P("sta", "gx", "gy", None)
    return jax.shard_map(
        on_device, mesh=mesh, in_specs=in_specs, out_specs=out_specs, check_vma=False
    )
```

```python
import math

import jax
import jax.numpy as jnp
from jax import lax
from jax.sharding import PartitionSpec as P

TIMES = 2
LINK_INV_Z = jnp.bfloat16
TAIL_CHUNKS = 2
FRONT_CHUNKS = 1
GROUPS = 8
NOISE_POWER = 0.25
HIGHEST = lax.Precision.HIGHEST
DFT = lax.Precision.HIGH


def station_counts(station_group):
    labels = jnp.arange(GROUPS, dtype=jnp.int32)
    onehot = (station_group[:, None] == labels[None, :]).astype(jnp.float32)
    totals = jnp.sum(onehot, axis=0)
    return jnp.dot(onehot, totals, precision=HIGHEST)


def angles(rows, cols, length):
    product = rows[:, None] * cols[None, :] % length
    return product.astype(jnp.float32) * (2.0 * math.pi / length)


def local_coefficients(record, shifts, per_station):
    trace = record.shape[1]
    samples = jnp.arange(trace, dtype=jnp.int32)
    times = jnp.arange(TIMES, dtype=jnp.int32)
    positions = shifts[:, None, :] + times[None, :, None]
    hit = positions[:, :, :, None] == samples[None, None, None, :]
    values = jnp.sum(jnp.where(hit, record[:, None, None, :], 0.0), axis=3)
    scaled = values / per_station[:, None, None]
    return jnp.transpose(scaled, (1, 2, 0)).astype(jnp.bfloat16)


def complex_block(rows, cols, length, sign, scale):
    ang = angles(rows, cols, length)
    cos, sin = jnp.cos(ang) * scale, jnp.sin(ang) * scale
    if sign < 0:
        return jnp.stack([jnp.stack([cos, -sin], 1), jnp.stack([sin, cos], 1)], 0)
    return jnp.stack([jnp.stack([cos, sin], 1), jnp.stack([-sin, cos], 1)], 0)


def mirrored_psf(psf_real, psf_imag, k_sta, n_gx, n_gy, half, barrier=None):
    both = jnp.stack([psf_real, psf_imag])
    nz, bb, cb = both.shape[1], both.shape[2], both.shape[3]
    n = n_gx * n_gy

    def send(piece, di, dj):
        pairs = [(q * n + i * n_gy + j, (1 - q) * n + ((di - i) % n_gx) * n_gy + (dj - j) % n_gy)
                 for q in range(2) for i in range(n_gx) for j in range(n_gy)]
        return lax.ppermute(piece, ("sta", "gx", "gy"), pairs)

    rows = lax.dynamic_slice_in_dim(both, half - (half - 1) * (1 - k_sta), half, axis=2)
    main = send(rows, n_gx - 1, n_gy - 1)
    col = send(rows[:, :, :, :1], n_gx - 1, n_gy)
    row = send(both[:, :, :1], n_gx, n_gy - 1)
    corner = send(both[:, :, :1, :1], n_gx, n_gy)
    window = jnp.concatenate(
        [jnp.concatenate([main, col], axis=3), jnp.concatenate([row, corner], axis=3)], axis=2
    )
    ia = jnp.arange(nz, dtype=jnp.int32)
    flip_a = (ia[:, None] == (nz - ia[None, :]) % nz).astype(jnp.float32)
    it = jnp.arange(half + 1, dtype=jnp.int32)[:, None]
    tb = jnp.arange(half, dtype=jnp.int32)[None, :]
    flip_t = (it == half - 1 - tb + 1 - k_sta).astype(jnp.float32)
    iu = jnp.arange(cb + 1, dtype=jnp.int32)[:, None]
    uc = jnp.arange(cb, dtype=jnp.int32)[None, :]
    flip_u = (iu == cb - uc).astype(jnp.float32)
    window = lax.optimization_barrier(window) if barrier is None else lax.optimization_barrier((window, barrier))
    window, barrier = window if isinstance(window, tuple) else (window, None)
    out = jnp.einsum("rxyz,zc->rxyc", window, flip_u, precision=HIGHEST)
    out = jnp.einsum("rxyc,yb->rxbc", out, flip_t, precision=HIGHEST)
    return jnp.einsum("rxbc,xa->rabc", out, flip_a, precision=HIGHEST), barrier


def on_device(record, shifts, station_group, weights, psf_real, psf_imag):
    n_sta = lax.axis_size("sta")
    n_gx = lax.axis_size("gx")
    n_gy = lax.axis_size("gy")
    k_sta = lax.axis_index("sta")
    per_station = station_counts(station_group)
    own = weights.shape[0]
    depth = shifts.shape[1]
    rows = weights.shape[1]
    width = weights.shape[2]
    nz = depth * n_gx
    nx = rows * n_gy
    cb = width // n_gy
    bb = nx // n_gx
    zh = depth // n_sta
    bh = bb // n_sta
    n_grp = n_gx * n_sta
    pairs = [(i, (i + 1) % n_sta) for i in range(n_sta)]

    start = k_sta * own
    rec = lax.dynamic_slice_in_dim(record, start, own, 0)
    sh = lax.dynamic_slice_in_dim(shifts, start, own, 0)
    cnt = lax.dynamic_slice_in_dim(per_station, start, own, 0)
    coef = local_coefficients(rec, sh, cnt)
    flat_weights = weights.reshape(own, rows * width)

    def half_field(first):
        part = lax.dynamic_slice_in_dim(coef, first, zh, axis=1).reshape(TIMES * zh, own)
        return jnp.dot(part, flat_weights, preferred_element_type=jnp.float32).reshape(
            TIMES, zh, rows, width)

    send = half_field((1 - k_sta) * zh)
    send, psf_real, psf_imag = lax.optimization_barrier((send, psf_real, psf_imag))
    keep = half_field(k_sta * zh)

    iy = jnp.arange(width, dtype=jnp.int32)
    ix = jnp.arange(nx, dtype=jnp.int32)
    iz = jnp.arange(nz, dtype=jnp.int32)
    ty = complex_block(iy, iy, width, -1, 1.0).reshape(2, width, 2, n_gy, cb)
    tx = complex_block(ix, ix, nx, -1, 1.0).reshape(2, n_gy, rows, 2, n_grp, bh)
    tz = complex_block(iz, iz, nz, -1, 1.0).reshape(2, n_grp, zh, 2, nz)

    zf = zh // FRONT_CHUNKS
    s3 = None
    recv = None
    for k in range(FRONT_CHUNKS):
        piece = send[:, k * zf:(k + 1) * zf]
        if recv is not None:
            piece, _ = lax.optimization_barrier((piece, recv))
        recv = lax.ppermute(piece, "sta", pairs)
        field = keep[:, k * zf:(k + 1) * zf] + recv
        if k == FRONT_CHUNKS - 1:
            mirror, field = mirrored_psf(psf_real, psf_imag, k_sta, n_gx, n_gy, bh, field)
        s1 = jnp.einsum("szxy,syrjc->jrzxc", field, ty, precision=DFT)
        s1 = lax.all_to_all(s1, "gy", 0, 0, tiled=True)
        s2 = jnp.einsum("jszxc,sjxrLb->Lrbzc", s1, tx, precision=DFT)
        s2 = lax.all_to_all(s2, ("gx", "sta"), 0, 0, tiled=True)
        part = jnp.einsum("Lsbzc,sLzra->rabc", s2, tz[:, :, k * zf:(k + 1) * zf], precision=DFT)
        s3 = part if s3 is None else s3 + part

    pr = lax.dynamic_slice_in_dim(psf_real, k_sta * bh, bh, axis=1)
    pi = lax.dynamic_slice_in_dim(psf_imag, k_sta * bh, bh, axis=1)
    pw = pr * pr + pi * pi + NOISE_POWER
    mr, mi = mirror[0], mirror[1]
    mw = mr * mr + mi * mi + NOISE_POWER
    we_re = 0.5 * (pr / pw + mr / mw)
    we_im = 0.5 * (mi / mw - pi / pw)
    h_re = we_re * s3[0] - we_im * s3[1]
    h_im = we_re * s3[1] + we_im * s3[0]
    filt = jnp.stack([h_re, h_im])

    tzi = complex_block(iz, iz, nz, 1, 1.0 / nz).reshape(2, nz, 2, n_grp, zh)
    g1 = jnp.einsum("sabc,sarLz->Lrzbc", filt, tzi, precision=DFT)
    if LINK_INV_Z is not None:
        g1 = g1.astype(LINK_INV_Z)
    g1 = lax.all_to_all(g1, ("gx", "sta"), 0, 0, tiled=True).astype(jnp.float32)
    txi = complex_block(ix, ix, nx, 1, 1.0 / nx).reshape(2, n_grp, bh, 2, n_gy, rows)
    tyi = complex_block(iy, iy, width, 1, 1.0 / width).reshape(2, n_gy, cb, 2, width)
    zt = zh // TAIL_CHUNKS
    mines, others = [], []
    for k in range(TAIL_CHUNKS):
        g2 = jnp.einsum("Lszbc,sLbrjx->jrzxc", g1[:, :, k * zt:(k + 1) * zt], txi, precision=DFT)
        g2 = lax.all_to_all(g2, "gy", 0, 0, tiled=True)
        both = jnp.einsum("jszxc,sjcry->rzxy", g2, tyi, precision=DFT)
        mines.append(lax.dynamic_index_in_dim(both, k_sta, 0, keepdims=False))
        others.append(lax.ppermute(
            lax.dynamic_index_in_dim(both, 1 - k_sta, 0, keepdims=False), "sta", pairs))
    mine = jnp.concatenate(mines, axis=0)
    other = jnp.concatenate(others, axis=0)
    first = jnp.where(k_sta == 0, mine, other)
    second = jnp.where(k_sta == 0, other, mine)
    return jnp.concatenate([first, second], axis=0)[None]


def solution(mesh):
    in_specs = (
        P(),
        P(None, "gx"),
        P(),
        P("sta", "gy", None),
        P(None, "gx", "gy"),
        P(None, "gx", "gy"),
    )
    out_specs = P("sta", "gx", "gy", None)
    return jax.shard_map(
        on_device, mesh=mesh, in_specs=in_specs, out_specs=out_specs, check_vma=False
    )
```

```python
import math

import jax
import jax.numpy as jnp
from jax import lax
from jax.sharding import PartitionSpec as P

TIMES = 2
LINK_INV_Z = jnp.bfloat16
TAIL_CHUNKS = 2
GROUPS = 8
NOISE_POWER = 0.25
HIGHEST = lax.Precision.HIGHEST
DFT = lax.Precision.HIGH


def station_counts(station_group):
    labels = jnp.arange(GROUPS, dtype=jnp.int32)
    onehot = (station_group[:, None] == labels[None, :]).astype(jnp.float32)
    totals = jnp.sum(onehot, axis=0)
    return jnp.dot(onehot, totals, precision=HIGHEST)


def angles(rows, cols, length):
    product = rows[:, None] * cols[None, :] % length
    return product.astype(jnp.float32) * (2.0 * math.pi / length)


def local_coefficients(record, shifts, per_station):
    trace = record.shape[1]
    samples = jnp.arange(trace, dtype=jnp.int32)
    times = jnp.arange(TIMES, dtype=jnp.int32)
    positions = shifts[:, None, :] + times[None, :, None]
    hit = positions[:, :, :, None] == samples[None, None, None, :]
    values = jnp.sum(jnp.where(hit, record[:, None, None, :], 0.0), axis=3)
    scaled = values / per_station[:, None, None]
    return jnp.transpose(scaled, (1, 2, 0)).astype(jnp.bfloat16)


def complex_block(rows, cols, length, sign, scale):
    ang = angles(rows, cols, length)
    cos, sin = jnp.cos(ang) * scale, jnp.sin(ang) * scale
    if sign < 0:
        return jnp.stack([jnp.stack([cos, -sin], 1), jnp.stack([sin, cos], 1)], 0)
    return jnp.stack([jnp.stack([cos, sin], 1), jnp.stack([-sin, cos], 1)], 0)


def mirrored_psf(psf_real, psf_imag, k_sta, n_gx, n_gy, half, barrier=None):
    both = jnp.stack([psf_real, psf_imag])
    nz, bb, cb = both.shape[1], both.shape[2], both.shape[3]
    n = n_gx * n_gy

    def send(piece, di, dj):
        pairs = [(q * n + i * n_gy + j, (1 - q) * n + ((di - i) % n_gx) * n_gy + (dj - j) % n_gy)
                 for q in range(2) for i in range(n_gx) for j in range(n_gy)]
        return lax.ppermute(piece, ("sta", "gx", "gy"), pairs)

    rows = lax.dynamic_slice_in_dim(both, half - (half - 1) * (1 - k_sta), half, axis=2)
    main = send(rows, n_gx - 1, n_gy - 1)
    col = send(rows[:, :, :, :1], n_gx - 1, n_gy)
    row = send(both[:, :, :1], n_gx, n_gy - 1)
    corner = send(both[:, :, :1, :1], n_gx, n_gy)
    window = jnp.concatenate(
        [jnp.concatenate([main, col], axis=3), jnp.concatenate([row, corner], axis=3)], axis=2
    )
    ia = jnp.arange(nz, dtype=jnp.int32)
    flip_a = (ia[:, None] == (nz - ia[None, :]) % nz).astype(jnp.float32)
    it = jnp.arange(half + 1, dtype=jnp.int32)[:, None]
    tb = jnp.arange(half, dtype=jnp.int32)[None, :]
    flip_t = (it == half - 1 - tb + 1 - k_sta).astype(jnp.float32)
    iu = jnp.arange(cb + 1, dtype=jnp.int32)[:, None]
    uc = jnp.arange(cb, dtype=jnp.int32)[None, :]
    flip_u = (iu == cb - uc).astype(jnp.float32)
    window = lax.optimization_barrier(window) if barrier is None else lax.optimization_barrier((window, barrier))
    window, barrier = window if isinstance(window, tuple) else (window, None)
    out = jnp.einsum("rxyz,zc->rxyc", window, flip_u, precision=HIGHEST)
    out = jnp.einsum("rxyc,yb->rxbc", out, flip_t, precision=HIGHEST)
    return jnp.einsum("rxbc,xa->rabc", out, flip_a, precision=HIGHEST), barrier


def on_device(record, shifts, station_group, weights, psf_real, psf_imag):
    n_sta = lax.axis_size("sta")
    n_gx = lax.axis_size("gx")
    n_gy = lax.axis_size("gy")
    k_sta = lax.axis_index("sta")
    per_station = station_counts(station_group)
    own = weights.shape[0]
    depth = shifts.shape[1]
    rows = weights.shape[1]
    width = weights.shape[2]
    nz = depth * n_gx
    nx = rows * n_gy
    cb = width // n_gy
    bb = nx // n_gx
    zh = depth // n_sta
    bh = bb // n_sta
    n_grp = n_gx * n_sta
    pairs = [(i, (i + 1) % n_sta) for i in range(n_sta)]

    start = k_sta * own
    rec = lax.dynamic_slice_in_dim(record, start, own, 0)
    sh = lax.dynamic_slice_in_dim(shifts, start, own, 0)
    cnt = lax.dynamic_slice_in_dim(per_station, start, own, 0)
    coef = local_coefficients(rec, sh, cnt).reshape(TIMES * depth, own)
    partial = jnp.dot(
        coef, weights.reshape(own, rows * width), preferred_element_type=jnp.float32
    ).reshape(TIMES, depth, rows, width)
    keep = lax.dynamic_slice_in_dim(partial, k_sta * zh, zh, axis=1)
    send = lax.dynamic_slice_in_dim(partial, (1 - k_sta) * zh, zh, axis=1)
    field = keep + lax.ppermute(send, "sta", pairs)

    iy = jnp.arange(width, dtype=jnp.int32)
    ix = jnp.arange(nx, dtype=jnp.int32)
    iz = jnp.arange(nz, dtype=jnp.int32)
    ty = complex_block(iy, iy, width, -1, 1.0).reshape(2, width, 2, n_gy, cb)
    s1 = jnp.einsum("szxy,syrjc->jrzxc", field, ty, precision=DFT)
    s1 = lax.all_to_all(s1, "gy", 0, 0, tiled=True)
    tx = complex_block(ix, ix, nx, -1, 1.0).reshape(2, n_gy, rows, 2, n_grp, bh)
    s2 = jnp.einsum("jszxc,sjxrLb->Lrbzc", s1, tx, precision=DFT)
    s2 = lax.all_to_all(s2, ("gx", "sta"), 0, 0, tiled=True)
    mirror, s2 = mirrored_psf(psf_real, psf_imag, k_sta, n_gx, n_gy, bh, s2)
    tz = complex_block(iz, iz, nz, -1, 1.0).reshape(2, n_grp, zh, 2, nz)
    s3 = jnp.einsum("Lsbzc,sLzra->rabc", s2, tz, precision=DFT)

    pr = lax.dynamic_slice_in_dim(psf_real, k_sta * bh, bh, axis=1)
    pi = lax.dynamic_slice_in_dim(psf_imag, k_sta * bh, bh, axis=1)
    pw = pr * pr + pi * pi + NOISE_POWER
    mr, mi = mirror[0], mirror[1]
    mw = mr * mr + mi * mi + NOISE_POWER
    we_re = 0.5 * (pr / pw + mr / mw)
    we_im = 0.5 * (mi / mw - pi / pw)
    h_re = we_re * s3[0] - we_im * s3[1]
    h_im = we_re * s3[1] + we_im * s3[0]
    filt = jnp.stack([h_re, h_im])

    tzi = complex_block(iz, iz, nz, 1, 1.0 / nz).reshape(2, nz, 2, n_grp, zh)
    g1 = jnp.einsum("sabc,sarLz->Lrzbc", filt, tzi, precision=DFT)
    if LINK_INV_Z is not None:
        g1 = g1.astype(LINK_INV_Z)
    g1 = lax.all_to_all(g1, ("gx", "sta"), 0, 0, tiled=True).astype(jnp.float32)
    txi = complex_block(ix, ix, nx, 1, 1.0 / nx).reshape(2, n_grp, bh, 2, n_gy, rows)
    tyi = complex_block(iy, iy, width, 1, 1.0 / width).reshape(2, n_gy, cb, 2, width)
    zt = zh // TAIL_CHUNKS
    mines, others = [], []
    for k in range(TAIL_CHUNKS):
        g2 = jnp.einsum("Lszbc,sLbrjx->jrzxc", g1[:, :, k * zt:(k + 1) * zt], txi, precision=DFT)
        g2 = lax.all_to_all(g2, "gy", 0, 0, tiled=True)
        both = jnp.einsum("jszxc,sjcry->rzxy", g2, tyi, precision=DFT)
        mines.append(lax.dynamic_index_in_dim(both, k_sta, 0, keepdims=False))
        others.append(lax.ppermute(
            lax.dynamic_index_in_dim(both, 1 - k_sta, 0, keepdims=False), "sta", pairs))
    mine = jnp.concatenate(mines, axis=0)
    other = jnp.concatenate(others, axis=0)
    first = jnp.where(k_sta == 0, mine, other)
    second = jnp.where(k_sta == 0, other, mine)
    return jnp.concatenate([first, second], axis=0)[None]


def solution(mesh):
    in_specs = (
        P(),
        P(None, "gx"),
        P(),
        P("sta", "gy", None),
        P(None, "gx", "gy"),
        P(None, "gx", "gy"),
    )
    out_specs = P("sta", "gx", "gy", None)
    return jax.shard_map(
        on_device, mesh=mesh, in_specs=in_specs, out_specs=out_specs, check_vma=False
    )
```

```python
import math

import jax
import jax.numpy as jnp
from jax import lax
from jax.sharding import PartitionSpec as P

TIMES = 2
LINK_INV_Z = jnp.bfloat16
TAIL_CHUNKS = 2
FRONT_CHUNKS = 1
GROUPS = 8
NOISE_POWER = 0.25
HIGHEST = lax.Precision.HIGHEST
DFT = lax.Precision.HIGH


def station_counts(station_group):
    labels = jnp.arange(GROUPS, dtype=jnp.int32)
    onehot = (station_group[:, None] == labels[None, :]).astype(jnp.float32)
    totals = jnp.sum(onehot, axis=0)
    return jnp.dot(onehot, totals, precision=HIGHEST)


def angles(rows, cols, length):
    product = rows[:, None] * cols[None, :] % length
    return product.astype(jnp.float32) * (2.0 * math.pi / length)


def local_coefficients(record, shifts, per_station):
    trace = record.shape[1]
    samples = jnp.arange(trace, dtype=jnp.int32)
    times = jnp.arange(TIMES, dtype=jnp.int32)
    positions = shifts[:, None, :] + times[None, :, None]
    hit = positions[:, :, :, None] == samples[None, None, None, :]
    values = jnp.sum(jnp.where(hit, record[:, None, None, :], 0.0), axis=3)
    scaled = values / per_station[:, None, None]
    return jnp.transpose(scaled, (1, 2, 0)).astype(jnp.bfloat16)


def complex_block(rows, cols, length, sign, scale):
    ang = angles(rows, cols, length)
    cos, sin = jnp.cos(ang) * scale, jnp.sin(ang) * scale
    if sign < 0:
        return jnp.stack([jnp.stack([cos, -sin], 1), jnp.stack([sin, cos], 1)], 0)
    return jnp.stack([jnp.stack([cos, sin], 1), jnp.stack([-sin, cos], 1)], 0)


def mirrored_psf(psf_real, psf_imag, k_sta, n_gx, n_gy, half, barrier=None):
    both = jnp.stack([psf_real, psf_imag])
    nz, bb, cb = both.shape[1], both.shape[2], both.shape[3]
    n = n_gx * n_gy

    def send(piece, di, dj):
        pairs = [(q * n + i * n_gy + j, (1 - q) * n + ((di - i) % n_gx) * n_gy + (dj - j) % n_gy)
                 for q in range(2) for i in range(n_gx) for j in range(n_gy)]
        return lax.ppermute(piece, ("sta", "gx", "gy"), pairs)

    rows = lax.dynamic_slice_in_dim(both, half - (half - 1) * (1 - k_sta), half, axis=2)
    main = send(rows, n_gx - 1, n_gy - 1)
    col = send(rows[:, :, :, :1], n_gx - 1, n_gy)
    row = send(both[:, :, :1], n_gx, n_gy - 1)
    corner = send(both[:, :, :1, :1], n_gx, n_gy)
    window = jnp.concatenate(
        [jnp.concatenate([main, col], axis=3), jnp.concatenate([row, corner], axis=3)], axis=2
    )
    ia = jnp.arange(nz, dtype=jnp.int32)
    flip_a = (ia[:, None] == (nz - ia[None, :]) % nz).astype(jnp.float32)
    it = jnp.arange(half + 1, dtype=jnp.int32)[:, None]
    tb = jnp.arange(half, dtype=jnp.int32)[None, :]
    flip_t = (it == half - 1 - tb + 1 - k_sta).astype(jnp.float32)
    iu = jnp.arange(cb + 1, dtype=jnp.int32)[:, None]
    uc = jnp.arange(cb, dtype=jnp.int32)[None, :]
    flip_u = (iu == cb - uc).astype(jnp.float32)
    window = lax.optimization_barrier(window) if barrier is None else lax.optimization_barrier((window, barrier))
    window, barrier = window if isinstance(window, tuple) else (window, None)
    out = jnp.einsum("rxyz,zc->rxyc", window, flip_u, precision=HIGHEST)
    out = jnp.einsum("rxyc,yb->rxbc", out, flip_t, precision=HIGHEST)
    return jnp.einsum("rxbc,xa->rabc", out, flip_a, precision=HIGHEST), barrier


def on_device(record, shifts, station_group, weights, psf_real, psf_imag):
    n_sta = lax.axis_size("sta")
    n_gx = lax.axis_size("gx")
    n_gy = lax.axis_size("gy")
    k_sta = lax.axis_index("sta")
    per_station = station_counts(station_group)
    own = weights.shape[0]
    depth = shifts.shape[1]
    rows = weights.shape[1]
    width = weights.shape[2]
    nz = depth * n_gx
    nx = rows * n_gy
    cb = width // n_gy
    bb = nx // n_gx
    zh = depth // n_sta
    bh = bb // n_sta
    n_grp = n_gx * n_sta
    pairs = [(i, (i + 1) % n_sta) for i in range(n_sta)]

    start = k_sta * own
    rec = lax.dynamic_slice_in_dim(record, start, own, 0)
    sh = lax.dynamic_slice_in_dim(shifts, start, own, 0)
    cnt = lax.dynamic_slice_in_dim(per_station, start, own, 0)
    coef = local_coefficients(rec, sh, cnt)
    flat_weights = weights.reshape(own, rows * width)

    def half_field(first):
        part = lax.dynamic_slice_in_dim(coef, first, zh, axis=1).reshape(TIMES * zh, own)
        return jnp.dot(part, flat_weights, preferred_element_type=jnp.float32).reshape(
            TIMES, zh, rows, width)

    send = half_field((1 - k_sta) * zh)
    keep = half_field(k_sta * zh)

    iy = jnp.arange(width, dtype=jnp.int32)
    ix = jnp.arange(nx, dtype=jnp.int32)
    iz = jnp.arange(nz, dtype=jnp.int32)
    ty = complex_block(iy, iy, width, -1, 1.0).reshape(2, width, 2, n_gy, cb)
    tx = complex_block(ix, ix, nx, -1, 1.0).reshape(2, n_gy, rows, 2, n_grp, bh)
    tz = complex_block(iz, iz, nz, -1, 1.0).reshape(2, n_grp, zh, 2, nz)

    zf = zh // FRONT_CHUNKS
    s3 = None
    recv = None
    for k in range(FRONT_CHUNKS):
        piece = send[:, k * zf:(k + 1) * zf]
        if recv is not None:
            piece, _ = lax.optimization_barrier((piece, recv))
        recv = lax.ppermute(piece, "sta", pairs)
        field = keep[:, k * zf:(k + 1) * zf] + recv
        if k == FRONT_CHUNKS - 1:
            mirror, field = mirrored_psf(psf_real, psf_imag, k_sta, n_gx, n_gy, bh, field)
        s1 = jnp.einsum("szxy,syrjc->jrzxc", field, ty, precision=DFT)
        s1 = lax.all_to_all(s1, "gy", 0, 0, tiled=True)
        s2 = jnp.einsum("jszxc,sjxrLb->Lrbzc", s1, tx, precision=DFT)
        s2 = lax.all_to_all(s2, ("gx", "sta"), 0, 0, tiled=True)
        part = jnp.einsum("Lsbzc,sLzra->rabc", s2, tz[:, :, k * zf:(k + 1) * zf], precision=DFT)
        s3 = part if s3 is None else s3 + part

    pr = lax.dynamic_slice_in_dim(psf_real, k_sta * bh, bh, axis=1)
    pi = lax.dynamic_slice_in_dim(psf_imag, k_sta * bh, bh, axis=1)
    pw = pr * pr + pi * pi + NOISE_POWER
    mr, mi = mirror[0], mirror[1]
    mw = mr * mr + mi * mi + NOISE_POWER
    we_re = 0.5 * (pr / pw + mr / mw)
    we_im = 0.5 * (mi / mw - pi / pw)
    h_re = we_re * s3[0] - we_im * s3[1]
    h_im = we_re * s3[1] + we_im * s3[0]
    filt = jnp.stack([h_re, h_im])

    tzi = complex_block(iz, iz, nz, 1, 1.0 / nz).reshape(2, nz, 2, n_grp, zh)
    g1 = jnp.einsum("sabc,sarLz->Lrzbc", filt, tzi, precision=DFT)
    if LINK_INV_Z is not None:
        g1 = g1.astype(LINK_INV_Z)
    g1 = lax.all_to_all(g1, ("gx", "sta"), 0, 0, tiled=True).astype(jnp.float32)
    txi = complex_block(ix, ix, nx, 1, 1.0 / nx).reshape(2, n_grp, bh, 2, n_gy, rows)
    tyi = complex_block(iy, iy, width, 1, 1.0 / width).reshape(2, n_gy, cb, 2, width)
    zt = zh // TAIL_CHUNKS
    mines, others = [], []
    for k in range(TAIL_CHUNKS):
        g2 = jnp.einsum("Lszbc,sLbrjx->jrzxc", g1[:, :, k * zt:(k + 1) * zt], txi, precision=DFT)
        g2 = lax.all_to_all(g2, "gy", 0, 0, tiled=True)
        both = jnp.einsum("jszxc,sjcry->rzxy", g2, tyi, precision=DFT)
        mines.append(lax.dynamic_index_in_dim(both, k_sta, 0, keepdims=False))
        others.append(lax.ppermute(
            lax.dynamic_index_in_dim(both, 1 - k_sta, 0, keepdims=False), "sta", pairs))
    mine = jnp.concatenate(mines, axis=0)
    other = jnp.concatenate(others, axis=0)
    first = jnp.where(k_sta == 0, mine, other)
    second = jnp.where(k_sta == 0, other, mine)
    return jnp.concatenate([first, second], axis=0)[None]


def solution(mesh):
    in_specs = (
        P(),
        P(None, "gx"),
        P(),
        P("sta", "gy", None),
        P(None, "gx", "gy"),
        P(None, "gx", "gy"),
    )
    out_specs = P("sta", "gx", "gy", None)
    return jax.shard_map(
        on_device, mesh=mesh, in_specs=in_specs, out_specs=out_specs, check_vma=False
    )
```

```python
import math

import jax
import jax.numpy as jnp
from jax import lax
from jax.sharding import PartitionSpec as P

TIMES = 2
LINK_INV_Z = jnp.bfloat16
TAIL_CHUNKS = 4
GROUPS = 8
NOISE_POWER = 0.25
HIGHEST = lax.Precision.HIGHEST
DFT = lax.Precision.HIGH


def station_counts(station_group):
    labels = jnp.arange(GROUPS, dtype=jnp.int32)
    onehot = (station_group[:, None] == labels[None, :]).astype(jnp.float32)
    totals = jnp.sum(onehot, axis=0)
    return jnp.dot(onehot, totals, precision=HIGHEST)


def angles(rows, cols, length):
    product = rows[:, None] * cols[None, :] % length
    return product.astype(jnp.float32) * (2.0 * math.pi / length)


def local_coefficients(record, shifts, per_station):
    trace = record.shape[1]
    samples = jnp.arange(trace, dtype=jnp.int32)
    times = jnp.arange(TIMES, dtype=jnp.int32)
    positions = shifts[:, None, :] + times[None, :, None]
    hit = positions[:, :, :, None] == samples[None, None, None, :]
    values = jnp.sum(jnp.where(hit, record[:, None, None, :], 0.0), axis=3)
    scaled = values / per_station[:, None, None]
    return jnp.transpose(scaled, (1, 2, 0)).astype(jnp.bfloat16)


def complex_block(rows, cols, length, sign, scale):
    ang = angles(rows, cols, length)
    cos, sin = jnp.cos(ang) * scale, jnp.sin(ang) * scale
    if sign < 0:
        return jnp.stack([jnp.stack([cos, -sin], 1), jnp.stack([sin, cos], 1)], 0)
    return jnp.stack([jnp.stack([cos, sin], 1), jnp.stack([-sin, cos], 1)], 0)


def mirrored_psf(psf_real, psf_imag, k_sta, n_gx, n_gy, half, barrier=None):
    both = jnp.stack([psf_real, psf_imag])
    nz, bb, cb = both.shape[1], both.shape[2], both.shape[3]
    n = n_gx * n_gy

    def send(piece, di, dj):
        pairs = [(q * n + i * n_gy + j, (1 - q) * n + ((di - i) % n_gx) * n_gy + (dj - j) % n_gy)
                 for q in range(2) for i in range(n_gx) for j in range(n_gy)]
        return lax.ppermute(piece, ("sta", "gx", "gy"), pairs)

    rows = lax.dynamic_slice_in_dim(both, half - (half - 1) * (1 - k_sta), half, axis=2)
    main = send(rows, n_gx - 1, n_gy - 1)
    col = send(rows[:, :, :, :1], n_gx - 1, n_gy)
    row = send(both[:, :, :1], n_gx, n_gy - 1)
    corner = send(both[:, :, :1, :1], n_gx, n_gy)
    window = jnp.concatenate(
        [jnp.concatenate([main, col], axis=3), jnp.concatenate([row, corner], axis=3)], axis=2
    )
    ia = jnp.arange(nz, dtype=jnp.int32)
    flip_a = (ia[:, None] == (nz - ia[None, :]) % nz).astype(jnp.float32)
    it = jnp.arange(half + 1, dtype=jnp.int32)[:, None]
    tb = jnp.arange(half, dtype=jnp.int32)[None, :]
    flip_t = (it == half - 1 - tb + 1 - k_sta).astype(jnp.float32)
    iu = jnp.arange(cb + 1, dtype=jnp.int32)[:, None]
    uc = jnp.arange(cb, dtype=jnp.int32)[None, :]
    flip_u = (iu == cb - uc).astype(jnp.float32)
    window = lax.optimization_barrier(window) if barrier is None else lax.optimization_barrier((window, barrier))
    window, barrier = window if isinstance(window, tuple) else (window, None)
    out = jnp.einsum("rxyz,zc->rxyc", window, flip_u, precision=HIGHEST)
    out = jnp.einsum("rxyc,yb->rxbc", out, flip_t, precision=HIGHEST)
    return jnp.einsum("rxbc,xa->rabc", out, flip_a, precision=HIGHEST), barrier


def on_device(record, shifts, station_group, weights, psf_real, psf_imag):
    n_sta = lax.axis_size("sta")
    n_gx = lax.axis_size("gx")
    n_gy = lax.axis_size("gy")
    k_sta = lax.axis_index("sta")
    per_station = station_counts(station_group)
    own = weights.shape[0]
    depth = shifts.shape[1]
    rows = weights.shape[1]
    width = weights.shape[2]
    nz = depth * n_gx
    nx = rows * n_gy
    cb = width // n_gy
    bb = nx // n_gx
    zh = depth // n_sta
    bh = bb // n_sta
    n_grp = n_gx * n_sta
    pairs = [(i, (i + 1) % n_sta) for i in range(n_sta)]

    start = k_sta * own
    rec = lax.dynamic_slice_in_dim(record, start, own, 0)
    sh = lax.dynamic_slice_in_dim(shifts, start, own, 0)
    cnt = lax.dynamic_slice_in_dim(per_station, start, own, 0)
    coef = local_coefficients(rec, sh, cnt).reshape(TIMES * depth, own)
    partial = jnp.dot(
        coef, weights.reshape(own, rows * width), preferred_element_type=jnp.float32
    ).reshape(TIMES, depth, rows, width)
    keep = lax.dynamic_slice_in_dim(partial, k_sta * zh, zh, axis=1)
    send = lax.dynamic_slice_in_dim(partial, (1 - k_sta) * zh, zh, axis=1)
    field = keep + lax.ppermute(send, "sta", pairs)
    mirror, field = mirrored_psf(psf_real, psf_imag, k_sta, n_gx, n_gy, bh, field)

    iy = jnp.arange(width, dtype=jnp.int32)
    ix = jnp.arange(nx, dtype=jnp.int32)
    iz = jnp.arange(nz, dtype=jnp.int32)
    ty = complex_block(iy, iy, width, -1, 1.0).reshape(2, width, 2, n_gy, cb)
    s1 = jnp.einsum("szxy,syrjc->jrzxc", field, ty, precision=DFT)
    s1 = lax.all_to_all(s1, "gy", 0, 0, tiled=True)
    tx = complex_block(ix, ix, nx, -1, 1.0).reshape(2, n_gy, rows, 2, n_grp, bh)
    s2 = jnp.einsum("jszxc,sjxrLb->Lrbzc", s1, tx, precision=DFT)
    s2 = lax.all_to_all(s2, ("gx", "sta"), 0, 0, tiled=True)
    tz = complex_block(iz, iz, nz, -1, 1.0).reshape(2, n_grp, zh, 2, nz)
    s3 = jnp.einsum("Lsbzc,sLzra->rabc", s2, tz, precision=DFT)

    pr = lax.dynamic_slice_in_dim(psf_real, k_sta * bh, bh, axis=1)
    pi = lax.dynamic_slice_in_dim(psf_imag, k_sta * bh, bh, axis=1)
    pw = pr * pr + pi * pi + NOISE_POWER
    mr, mi = mirror[0], mirror[1]
    mw = mr * mr + mi * mi + NOISE_POWER
    we_re = 0.5 * (pr / pw + mr / mw)
    we_im = 0.5 * (mi / mw - pi / pw)
    h_re = we_re * s3[0] - we_im * s3[1]
    h_im = we_re * s3[1] + we_im * s3[0]
    filt = jnp.stack([h_re, h_im])

    tzi = complex_block(iz, iz, nz, 1, 1.0 / nz).reshape(2, nz, 2, n_grp, zh)
    g1 = jnp.einsum("sabc,sarLz->Lrzbc", filt, tzi, precision=DFT)
    if LINK_INV_Z is not None:
        g1 = g1.astype(LINK_INV_Z)
    g1 = lax.all_to_all(g1, ("gx", "sta"), 0, 0, tiled=True).astype(jnp.float32)
    txi = complex_block(ix, ix, nx, 1, 1.0 / nx).reshape(2, n_grp, bh, 2, n_gy, rows)
    tyi = complex_block(iy, iy, width, 1, 1.0 / width).reshape(2, n_gy, cb, 2, width)
    zt = zh // TAIL_CHUNKS
    mines, others = [], []
    for k in range(TAIL_CHUNKS):
        g2 = jnp.einsum("Lszbc,sLbrjx->jrzxc", g1[:, :, k * zt:(k + 1) * zt], txi, precision=DFT)
        g2 = lax.all_to_all(g2, "gy", 0, 0, tiled=True)
        both = jnp.einsum("jszxc,sjcry->rzxy", g2, tyi, precision=DFT)
        mines.append(lax.dynamic_index_in_dim(both, k_sta, 0, keepdims=False))
        others.append(lax.ppermute(
            lax.dynamic_index_in_dim(both, 1 - k_sta, 0, keepdims=False), "sta", pairs))
    mine = jnp.concatenate(mines, axis=0)
    other = jnp.concatenate(others, axis=0)
    first = jnp.where(k_sta == 0, mine, other)
    second = jnp.where(k_sta == 0, other, mine)
    return jnp.concatenate([first, second], axis=0)[None]


def solution(mesh):
    in_specs = (
        P(),
        P(None, "gx"),
        P(),
        P("sta", "gy", None),
        P(None, "gx", "gy"),
        P(None, "gx", "gy"),
    )
    out_specs = P("sta", "gx", "gy", None)
    return jax.shard_map(
        on_device, mesh=mesh, in_specs=in_specs, out_specs=out_specs, check_vma=False
    )
```

```python
import math

import jax
import jax.numpy as jnp
from jax import lax
from jax.sharding import PartitionSpec as P
from jax.experimental.layout import Layout, with_layout_constraint

TIMES = 2
LINK_INV_Z = jnp.bfloat16
TAIL_CHUNKS = 2
GROUPS = 8
NOISE_POWER = 0.25
HIGHEST = lax.Precision.HIGHEST
DFT = lax.Precision.HIGH


def station_counts(station_group):
    labels = jnp.arange(GROUPS, dtype=jnp.int32)
    onehot = (station_group[:, None] == labels[None, :]).astype(jnp.float32)
    totals = jnp.sum(onehot, axis=0)
    return jnp.dot(onehot, totals, precision=HIGHEST)


def angles(rows, cols, length):
    product = rows[:, None] * cols[None, :] % length
    return product.astype(jnp.float32) * (2.0 * math.pi / length)


def local_coefficients(record, shifts, per_station):
    trace = record.shape[1]
    samples = jnp.arange(trace, dtype=jnp.int32)
    times = jnp.arange(TIMES, dtype=jnp.int32)
    positions = shifts[:, None, :] + times[None, :, None]
    hit = positions[:, :, :, None] == samples[None, None, None, :]
    values = jnp.sum(jnp.where(hit, record[:, None, None, :], 0.0), axis=3)
    scaled = values / per_station[:, None, None]
    return jnp.transpose(scaled, (1, 2, 0)).astype(jnp.bfloat16)


def complex_block(rows, cols, length, sign, scale):
    ang = angles(rows, cols, length)
    cos, sin = jnp.cos(ang) * scale, jnp.sin(ang) * scale
    if sign < 0:
        return jnp.stack([jnp.stack([cos, -sin], 1), jnp.stack([sin, cos], 1)], 0)
    return jnp.stack([jnp.stack([cos, sin], 1), jnp.stack([-sin, cos], 1)], 0)


def mirrored_psf(psf_real, psf_imag, k_sta, n_gx, n_gy, half, barrier=None):
    both = jnp.stack([psf_real, psf_imag])
    nz, bb, cb = both.shape[1], both.shape[2], both.shape[3]
    n = n_gx * n_gy

    def send(piece, di, dj):
        pairs = [(q * n + i * n_gy + j, (1 - q) * n + ((di - i) % n_gx) * n_gy + (dj - j) % n_gy)
                 for q in range(2) for i in range(n_gx) for j in range(n_gy)]
        piece = with_layout_constraint(piece, Layout(major_to_minor=tuple(range(piece.ndim))))
        got = lax.ppermute(piece, ("sta", "gx", "gy"), pairs)
        return with_layout_constraint(got, Layout(major_to_minor=tuple(range(got.ndim))))

    rows = lax.dynamic_slice_in_dim(both, half - (half - 1) * (1 - k_sta), half, axis=2)
    main = send(rows, n_gx - 1, n_gy - 1)
    col = send(rows[:, :, :, :1], n_gx - 1, n_gy)
    row = send(both[:, :, :1], n_gx, n_gy - 1)
    corner = send(both[:, :, :1, :1], n_gx, n_gy)
    window = jnp.concatenate(
        [jnp.concatenate([main, col], axis=3), jnp.concatenate([row, corner], axis=3)], axis=2
    )
    ia = jnp.arange(nz, dtype=jnp.int32)
    flip_a = (ia[:, None] == (nz - ia[None, :]) % nz).astype(jnp.float32)
    it = jnp.arange(half + 1, dtype=jnp.int32)[:, None]
    tb = jnp.arange(half, dtype=jnp.int32)[None, :]
    flip_t = (it == half - 1 - tb + 1 - k_sta).astype(jnp.float32)
    iu = jnp.arange(cb + 1, dtype=jnp.int32)[:, None]
    uc = jnp.arange(cb, dtype=jnp.int32)[None, :]
    flip_u = (iu == cb - uc).astype(jnp.float32)
    window = lax.optimization_barrier(window) if barrier is None else lax.optimization_barrier((window, barrier))
    window, barrier = window if isinstance(window, tuple) else (window, None)
    out = jnp.einsum("rxyz,zc->rxyc", window, flip_u, precision=HIGHEST)
    out = jnp.einsum("rxyc,yb->rxbc", out, flip_t, precision=HIGHEST)
    return jnp.einsum("rxbc,xa->rabc", out, flip_a, precision=HIGHEST), barrier


def on_device(record, shifts, station_group, weights, psf_real, psf_imag):
    n_sta = lax.axis_size("sta")
    n_gx = lax.axis_size("gx")
    n_gy = lax.axis_size("gy")
    k_sta = lax.axis_index("sta")
    per_station = station_counts(station_group)
    own = weights.shape[0]
    depth = shifts.shape[1]
    rows = weights.shape[1]
    width = weights.shape[2]
    nz = depth * n_gx
    nx = rows * n_gy
    cb = width // n_gy
    bb = nx // n_gx
    zh = depth // n_sta
    bh = bb // n_sta
    n_grp = n_gx * n_sta
    pairs = [(i, (i + 1) % n_sta) for i in range(n_sta)]

    start = k_sta * own
    rec = lax.dynamic_slice_in_dim(record, start, own, 0)
    sh = lax.dynamic_slice_in_dim(shifts, start, own, 0)
    cnt = lax.dynamic_slice_in_dim(per_station, start, own, 0)
    coef = local_coefficients(rec, sh, cnt).reshape(TIMES * depth, own)
    partial = jnp.dot(
        coef, weights.reshape(own, rows * width), preferred_element_type=jnp.float32
    ).reshape(TIMES, depth, rows, width)
    keep = lax.dynamic_slice_in_dim(partial, k_sta * zh, zh, axis=1)
    send = lax.dynamic_slice_in_dim(partial, (1 - k_sta) * zh, zh, axis=1)
    field = keep + lax.ppermute(send, "sta", pairs)
    mirror, field = mirrored_psf(psf_real, psf_imag, k_sta, n_gx, n_gy, bh, field)

    iy = jnp.arange(width, dtype=jnp.int32)
    ix = jnp.arange(nx, dtype=jnp.int32)
    iz = jnp.arange(nz, dtype=jnp.int32)
    ty = complex_block(iy, iy, width, -1, 1.0).reshape(2, width, 2, n_gy, cb)
    s1 = jnp.einsum("szxy,syrjc->jrzxc", field, ty, precision=DFT)
    s1 = lax.all_to_all(s1, "gy", 0, 0, tiled=True)
    tx = complex_block(ix, ix, nx, -1, 1.0).reshape(2, n_gy, rows, 2, n_grp, bh)
    s2 = jnp.einsum("jszxc,sjxrLb->Lrbzc", s1, tx, precision=DFT)
    s2 = lax.all_to_all(s2, ("gx", "sta"), 0, 0, tiled=True)
    tz = complex_block(iz, iz, nz, -1, 1.0).reshape(2, n_grp, zh, 2, nz)
    s3 = jnp.einsum("Lsbzc,sLzra->rabc", s2, tz, precision=DFT)

    pr = lax.dynamic_slice_in_dim(psf_real, k_sta * bh, bh, axis=1)
    pi = lax.dynamic_slice_in_dim(psf_imag, k_sta * bh, bh, axis=1)
    pw = pr * pr + pi * pi + NOISE_POWER
    mr, mi = mirror[0], mirror[1]
    mw = mr * mr + mi * mi + NOISE_POWER
    we_re = 0.5 * (pr / pw + mr / mw)
    we_im = 0.5 * (mi / mw - pi / pw)
    h_re = we_re * s3[0] - we_im * s3[1]
    h_im = we_re * s3[1] + we_im * s3[0]
    filt = jnp.stack([h_re, h_im])

    tzi = complex_block(iz, iz, nz, 1, 1.0 / nz).reshape(2, nz, 2, n_grp, zh)
    g1 = jnp.einsum("sabc,sarLz->Lrzbc", filt, tzi, precision=DFT)
    if LINK_INV_Z is not None:
        g1 = g1.astype(LINK_INV_Z)
    g1 = lax.all_to_all(g1, ("gx", "sta"), 0, 0, tiled=True).astype(jnp.float32)
    txi = complex_block(ix, ix, nx, 1, 1.0 / nx).reshape(2, n_grp, bh, 2, n_gy, rows)
    tyi = complex_block(iy, iy, width, 1, 1.0 / width).reshape(2, n_gy, cb, 2, width)
    zt = zh // TAIL_CHUNKS
    mines, others = [], []
    for k in range(TAIL_CHUNKS):
        g2 = jnp.einsum("Lszbc,sLbrjx->jrzxc", g1[:, :, k * zt:(k + 1) * zt], txi, precision=DFT)
        g2 = lax.all_to_all(g2, "gy", 0, 0, tiled=True)
        both = jnp.einsum("jszxc,sjcry->rzxy", g2, tyi, precision=DFT)
        mines.append(lax.dynamic_index_in_dim(both, k_sta, 0, keepdims=False))
        others.append(lax.ppermute(
            lax.dynamic_index_in_dim(both, 1 - k_sta, 0, keepdims=False), "sta", pairs))
    mine = jnp.concatenate(mines, axis=0)
    other = jnp.concatenate(others, axis=0)
    first = jnp.where(k_sta == 0, mine, other)
    second = jnp.where(k_sta == 0, other, mine)
    return jnp.concatenate([first, second], axis=0)[None]


def solution(mesh):
    in_specs = (
        P(),
        P(None, "gx"),
        P(),
        P("sta", "gy", None),
        P(None, "gx", "gy"),
        P(None, "gx", "gy"),
    )
    out_specs = P("sta", "gx", "gy", None)
    return jax.shard_map(
        on_device, mesh=mesh, in_specs=in_specs, out_specs=out_specs, check_vma=False
    )
```

```python
import math

import jax
import jax.numpy as jnp
from jax import lax
from jax.sharding import PartitionSpec as P
from jax.experimental.layout import Layout, with_layout_constraint

TIMES = 2
LINK_INV_Z = jnp.bfloat16
TAIL_CHUNKS = 2
GROUPS = 8
NOISE_POWER = 0.25
HIGHEST = lax.Precision.HIGHEST
DFT = lax.Precision.HIGH


def station_counts(station_group):
    labels = jnp.arange(GROUPS, dtype=jnp.int32)
    onehot = (station_group[:, None] == labels[None, :]).astype(jnp.float32)
    totals = jnp.sum(onehot, axis=0)
    return jnp.dot(onehot, totals, precision=HIGHEST)


def angles(rows, cols, length):
    product = rows[:, None] * cols[None, :] % length
    return product.astype(jnp.float32) * (2.0 * math.pi / length)


def local_coefficients(record, shifts, per_station):
    trace = record.shape[1]
    samples = jnp.arange(trace, dtype=jnp.int32)
    times = jnp.arange(TIMES, dtype=jnp.int32)
    positions = shifts[:, None, :] + times[None, :, None]
    hit = positions[:, :, :, None] == samples[None, None, None, :]
    values = jnp.sum(jnp.where(hit, record[:, None, None, :], 0.0), axis=3)
    scaled = values / per_station[:, None, None]
    return jnp.transpose(scaled, (1, 2, 0)).astype(jnp.bfloat16)


def complex_block(rows, cols, length, sign, scale):
    ang = angles(rows, cols, length)
    cos, sin = jnp.cos(ang) * scale, jnp.sin(ang) * scale
    if sign < 0:
        return jnp.stack([jnp.stack([cos, -sin], 1), jnp.stack([sin, cos], 1)], 0)
    return jnp.stack([jnp.stack([cos, sin], 1), jnp.stack([-sin, cos], 1)], 0)


def mirrored_psf(psf_real, psf_imag, k_sta, n_gx, n_gy, half, barrier=None):
    both = jnp.stack([psf_real, psf_imag])
    nz, bb, cb = both.shape[1], both.shape[2], both.shape[3]
    n = n_gx * n_gy

    def send(piece, di, dj):
        pairs = [(q * n + i * n_gy + j, (1 - q) * n + ((di - i) % n_gx) * n_gy + (dj - j) % n_gy)
                 for q in range(2) for i in range(n_gx) for j in range(n_gy)]
        piece = with_layout_constraint(piece, Layout(major_to_minor=tuple(range(piece.ndim))))
        got = lax.ppermute(piece, ("sta", "gx", "gy"), pairs)
        return with_layout_constraint(got, Layout(major_to_minor=tuple(range(got.ndim))))

    rows = lax.dynamic_slice_in_dim(both, half - (half - 1) * (1 - k_sta), half, axis=2)
    main = send(rows, n_gx - 1, n_gy - 1)
    col = send(rows[:, :, :, :1], n_gx - 1, n_gy)
    row = send(both[:, :, :1], n_gx, n_gy - 1)
    corner = send(both[:, :, :1, :1], n_gx, n_gy)
    window = jnp.concatenate(
        [jnp.concatenate([main, col], axis=3), jnp.concatenate([row, corner], axis=3)], axis=2
    )
    ia = jnp.arange(nz, dtype=jnp.int32)
    flip_a = (ia[:, None] == (nz - ia[None, :]) % nz).astype(jnp.float32)
    it = jnp.arange(half + 1, dtype=jnp.int32)[:, None]
    tb = jnp.arange(half, dtype=jnp.int32)[None, :]
    flip_t = (it == half - 1 - tb + 1 - k_sta).astype(jnp.float32)
    iu = jnp.arange(cb + 1, dtype=jnp.int32)[:, None]
    uc = jnp.arange(cb, dtype=jnp.int32)[None, :]
    flip_u = (iu == cb - uc).astype(jnp.float32)
    window = lax.optimization_barrier(window) if barrier is None else lax.optimization_barrier((window, barrier))
    window, barrier = window if isinstance(window, tuple) else (window, None)
    out = jnp.einsum("rxyz,zc->rxyc", window, flip_u, precision=HIGHEST)
    out = jnp.einsum("rxyc,yb->rxbc", out, flip_t, precision=HIGHEST)
    return jnp.einsum("rxbc,xa->rabc", out, flip_a, precision=HIGHEST), barrier


def on_device(record, shifts, station_group, weights, psf_real, psf_imag):
    n_sta = lax.axis_size("sta")
    n_gx = lax.axis_size("gx")
    n_gy = lax.axis_size("gy")
    k_sta = lax.axis_index("sta")
    per_station = station_counts(station_group)
    own = weights.shape[0]
    depth = shifts.shape[1]
    rows = weights.shape[1]
    width = weights.shape[2]
    nz = depth * n_gx
    nx = rows * n_gy
    cb = width // n_gy
    bb = nx // n_gx
    zh = depth // n_sta
    bh = bb // n_sta
    n_grp = n_gx * n_sta
    pairs = [(i, (i + 1) % n_sta) for i in range(n_sta)]

    start = k_sta * own
    rec = lax.dynamic_slice_in_dim(record, start, own, 0)
    sh = lax.dynamic_slice_in_dim(shifts, start, own, 0)
    cnt = lax.dynamic_slice_in_dim(per_station, start, own, 0)
    coef = local_coefficients(rec, sh, cnt)
    flat_weights = weights.reshape(own, rows * width)

    def half_field(first):
        part = lax.dynamic_slice_in_dim(coef, first, zh, axis=1).reshape(TIMES * zh, own)
        return jnp.dot(part, flat_weights, preferred_element_type=jnp.float32).reshape(
            TIMES, zh, rows, width)

    send = half_field((1 - k_sta) * zh)
    send, psf_real, psf_imag = lax.optimization_barrier((send, psf_real, psf_imag))
    keep = half_field(k_sta * zh)
    field = keep + lax.ppermute(send, "sta", pairs)
    mirror, field = mirrored_psf(psf_real, psf_imag, k_sta, n_gx, n_gy, bh, field)

    iy = jnp.arange(width, dtype=jnp.int32)
    ix = jnp.arange(nx, dtype=jnp.int32)
    iz = jnp.arange(nz, dtype=jnp.int32)
    ty = complex_block(iy, iy, width, -1, 1.0).reshape(2, width, 2, n_gy, cb)
    s1 = jnp.einsum("szxy,syrjc->jrzxc", field, ty, precision=DFT)
    s1 = lax.all_to_all(s1, "gy", 0, 0, tiled=True)
    tx = complex_block(ix, ix, nx, -1, 1.0).reshape(2, n_gy, rows, 2, n_grp, bh)
    s2 = jnp.einsum("jszxc,sjxrLb->Lrbzc", s1, tx, precision=DFT)
    s2 = lax.all_to_all(s2, ("gx", "sta"), 0, 0, tiled=True)
    tz = complex_block(iz, iz, nz, -1, 1.0).reshape(2, n_grp, zh, 2, nz)
    s3 = jnp.einsum("Lsbzc,sLzra->rabc", s2, tz, precision=DFT)

    pr = lax.dynamic_slice_in_dim(psf_real, k_sta * bh, bh, axis=1)
    pi = lax.dynamic_slice_in_dim(psf_imag, k_sta * bh, bh, axis=1)
    pw = pr * pr + pi * pi + NOISE_POWER
    mr, mi = mirror[0], mirror[1]
    mw = mr * mr + mi * mi + NOISE_POWER
    we_re = 0.5 * (pr / pw + mr / mw)
    we_im = 0.5 * (mi / mw - pi / pw)
    h_re = we_re * s3[0] - we_im * s3[1]
    h_im = we_re * s3[1] + we_im * s3[0]
    filt = jnp.stack([h_re, h_im])

    tzi = complex_block(iz, iz, nz, 1, 1.0 / nz).reshape(2, nz, 2, n_grp, zh)
    g1 = jnp.einsum("sabc,sarLz->Lrzbc", filt, tzi, precision=DFT)
    if LINK_INV_Z is not None:
        g1 = g1.astype(LINK_INV_Z)
    g1 = lax.all_to_all(g1, ("gx", "sta"), 0, 0, tiled=True).astype(jnp.float32)
    txi = complex_block(ix, ix, nx, 1, 1.0 / nx).reshape(2, n_grp, bh, 2, n_gy, rows)
    tyi = complex_block(iy, iy, width, 1, 1.0 / width).reshape(2, n_gy, cb, 2, width)
    zt = zh // TAIL_CHUNKS
    mines, others = [], []
    for k in range(TAIL_CHUNKS):
        g2 = jnp.einsum("Lszbc,sLbrjx->jrzxc", g1[:, :, k * zt:(k + 1) * zt], txi, precision=DFT)
        g2 = lax.all_to_all(g2, "gy", 0, 0, tiled=True)
        both = jnp.einsum("jszxc,sjcry->rzxy", g2, tyi, precision=DFT)
        mines.append(lax.dynamic_index_in_dim(both, k_sta, 0, keepdims=False))
        others.append(lax.ppermute(
            lax.dynamic_index_in_dim(both, 1 - k_sta, 0, keepdims=False), "sta", pairs))
    mine = jnp.concatenate(mines, axis=0)
    other = jnp.concatenate(others, axis=0)
    first = jnp.where(k_sta == 0, mine, other)
    second = jnp.where(k_sta == 0, other, mine)
    return jnp.concatenate([first, second], axis=0)[None]


def solution(mesh):
    in_specs = (
        P(),
        P(None, "gx"),
        P(),
        P("sta", "gy", None),
        P(None, "gx", "gy"),
        P(None, "gx", "gy"),
    )
    out_specs = P("sta", "gx", "gy", None)
    return jax.shard_map(
        on_device, mesh=mesh, in_specs=in_specs, out_specs=out_specs, check_vma=False
    )
```

```python
import math

import jax
import jax.numpy as jnp
from jax import lax
from jax.sharding import PartitionSpec as P

TIMES = 2
LINK_INV_Z = jnp.bfloat16
TAIL_CHUNKS = 2
GROUPS = 8
NOISE_POWER = 0.25
HIGHEST = lax.Precision.HIGHEST
DFT = lax.Precision.HIGH


def station_counts(station_group):
    labels = jnp.arange(GROUPS, dtype=jnp.int32)
    onehot = (station_group[:, None] == labels[None, :]).astype(jnp.float32)
    totals = jnp.sum(onehot, axis=0)
    return jnp.dot(onehot, totals, precision=HIGHEST)


def angles(rows, cols, length):
    product = rows[:, None] * cols[None, :] % length
    return product.astype(jnp.float32) * (2.0 * math.pi / length)


def local_coefficients(record, shifts, per_station):
    trace = record.shape[1]
    samples = jnp.arange(trace, dtype=jnp.int32)
    times = jnp.arange(TIMES, dtype=jnp.int32)
    positions = shifts[:, None, :] + times[None, :, None]
    hit = positions[:, :, :, None] == samples[None, None, None, :]
    values = jnp.sum(jnp.where(hit, record[:, None, None, :], 0.0), axis=3)
    scaled = values / per_station[:, None, None]
    return jnp.transpose(scaled, (1, 2, 0)).astype(jnp.bfloat16)


def complex_block(rows, cols, length, sign, scale):
    ang = angles(rows, cols, length)
    cos, sin = jnp.cos(ang) * scale, jnp.sin(ang) * scale
    if sign < 0:
        return jnp.stack([jnp.stack([cos, -sin], 1), jnp.stack([sin, cos], 1)], 0)
    return jnp.stack([jnp.stack([cos, sin], 1), jnp.stack([-sin, cos], 1)], 0)


def mirrored_psf(psf_real, psf_imag, k_sta, n_gx, n_gy, half, barrier=None):
    both = jnp.stack([psf_real, psf_imag])
    nz, bb, cb = both.shape[1], both.shape[2], both.shape[3]
    n = n_gx * n_gy

    def send(piece, di, dj):
        pairs = [(q * n + i * n_gy + j, (1 - q) * n + ((di - i) % n_gx) * n_gy + (dj - j) % n_gy)
                 for q in range(2) for i in range(n_gx) for j in range(n_gy)]
        return lax.ppermute(piece, ("sta", "gx", "gy"), pairs)

    rows = lax.dynamic_slice_in_dim(both, half - (half - 1) * (1 - k_sta), half, axis=2)
    main = send(rows, n_gx - 1, n_gy - 1)
    col = send(rows[:, :, :, :1], n_gx - 1, n_gy)
    row = send(both[:, :, :1], n_gx, n_gy - 1)
    corner = send(both[:, :, :1, :1], n_gx, n_gy)
    (main, col, row, corner), barrier = lax.optimization_barrier(((main, col, row, corner), barrier))
    window = jnp.concatenate(
        [jnp.concatenate([main, col], axis=3), jnp.concatenate([row, corner], axis=3)], axis=2
    )
    ia = jnp.arange(nz, dtype=jnp.int32)
    flip_a = (ia[:, None] == (nz - ia[None, :]) % nz).astype(jnp.float32)
    it = jnp.arange(half + 1, dtype=jnp.int32)[:, None]
    tb = jnp.arange(half, dtype=jnp.int32)[None, :]
    flip_t = (it == half - 1 - tb + 1 - k_sta).astype(jnp.float32)
    iu = jnp.arange(cb + 1, dtype=jnp.int32)[:, None]
    uc = jnp.arange(cb, dtype=jnp.int32)[None, :]
    flip_u = (iu == cb - uc).astype(jnp.float32)
    out = jnp.einsum("rxyz,zc->rxyc", window, flip_u, precision=HIGHEST)
    out = jnp.einsum("rxyc,yb->rxbc", out, flip_t, precision=HIGHEST)
    return jnp.einsum("rxbc,xa->rabc", out, flip_a, precision=HIGHEST), barrier


def on_device(record, shifts, station_group, weights, psf_real, psf_imag):
    n_sta = lax.axis_size("sta")
    n_gx = lax.axis_size("gx")
    n_gy = lax.axis_size("gy")
    k_sta = lax.axis_index("sta")
    per_station = station_counts(station_group)
    own = weights.shape[0]
    depth = shifts.shape[1]
    rows = weights.shape[1]
    width = weights.shape[2]
    nz = depth * n_gx
    nx = rows * n_gy
    cb = width // n_gy
    bb = nx // n_gx
    zh = depth // n_sta
    bh = bb // n_sta
    n_grp = n_gx * n_sta
    pairs = [(i, (i + 1) % n_sta) for i in range(n_sta)]

    start = k_sta * own
    rec = lax.dynamic_slice_in_dim(record, start, own, 0)
    sh = lax.dynamic_slice_in_dim(shifts, start, own, 0)
    cnt = lax.dynamic_slice_in_dim(per_station, start, own, 0)
    coef = local_coefficients(rec, sh, cnt).reshape(TIMES * depth, own)
    partial = jnp.dot(
        coef, weights.reshape(own, rows * width), preferred_element_type=jnp.float32
    ).reshape(TIMES, depth, rows, width)
    keep = lax.dynamic_slice_in_dim(partial, k_sta * zh, zh, axis=1)
    send = lax.dynamic_slice_in_dim(partial, (1 - k_sta) * zh, zh, axis=1)
    field = keep + lax.ppermute(send, "sta", pairs)
    mirror, field = mirrored_psf(psf_real, psf_imag, k_sta, n_gx, n_gy, bh, field)

    iy = jnp.arange(width, dtype=jnp.int32)
    ix = jnp.arange(nx, dtype=jnp.int32)
    iz = jnp.arange(nz, dtype=jnp.int32)
    ty = complex_block(iy, iy, width, -1, 1.0).reshape(2, width, 2, n_gy, cb)
    s1 = jnp.einsum("szxy,syrjc->jrzxc", field, ty, precision=DFT)
    s1 = lax.all_to_all(s1, "gy", 0, 0, tiled=True)
    tx = complex_block(ix, ix, nx, -1, 1.0).reshape(2, n_gy, rows, 2, n_grp, bh)
    s2 = jnp.einsum("jszxc,sjxrLb->Lrbzc", s1, tx, precision=DFT)
    s2 = lax.all_to_all(s2, ("gx", "sta"), 0, 0, tiled=True)
    tz = complex_block(iz, iz, nz, -1, 1.0).reshape(2, n_grp, zh, 2, nz)
    s3 = jnp.einsum("Lsbzc,sLzra->rabc", s2, tz, precision=DFT)

    pr = lax.dynamic_slice_in_dim(psf_real, k_sta * bh, bh, axis=1)
    pi = lax.dynamic_slice_in_dim(psf_imag, k_sta * bh, bh, axis=1)
    pw = pr * pr + pi * pi + NOISE_POWER
    mr, mi = mirror[0], mirror[1]
    mw = mr * mr + mi * mi + NOISE_POWER
    we_re = 0.5 * (pr / pw + mr / mw)
    we_im = 0.5 * (mi / mw - pi / pw)
    h_re = we_re * s3[0] - we_im * s3[1]
    h_im = we_re * s3[1] + we_im * s3[0]
    filt = jnp.stack([h_re, h_im])

    tzi = complex_block(iz, iz, nz, 1, 1.0 / nz).reshape(2, nz, 2, n_grp, zh)
    g1 = jnp.einsum("sabc,sarLz->Lrzbc", filt, tzi, precision=DFT)
    if LINK_INV_Z is not None:
        g1 = g1.astype(LINK_INV_Z)
    g1 = lax.all_to_all(g1, ("gx", "sta"), 0, 0, tiled=True).astype(jnp.float32)
    txi = complex_block(ix, ix, nx, 1, 1.0 / nx).reshape(2, n_grp, bh, 2, n_gy, rows)
    tyi = complex_block(iy, iy, width, 1, 1.0 / width).reshape(2, n_gy, cb, 2, width)
    zt = zh // TAIL_CHUNKS
    mines, others = [], []
    for k in range(TAIL_CHUNKS):
        g2 = jnp.einsum("Lszbc,sLbrjx->jrzxc", g1[:, :, k * zt:(k + 1) * zt], txi, precision=DFT)
        g2 = lax.all_to_all(g2, "gy", 0, 0, tiled=True)
        both = jnp.einsum("jszxc,sjcry->rzxy", g2, tyi, precision=DFT)
        mines.append(lax.dynamic_index_in_dim(both, k_sta, 0, keepdims=False))
        others.append(lax.ppermute(
            lax.dynamic_index_in_dim(both, 1 - k_sta, 0, keepdims=False), "sta", pairs))
    mine = jnp.concatenate(mines, axis=0)
    other = jnp.concatenate(others, axis=0)
    first = jnp.where(k_sta == 0, mine, other)
    second = jnp.where(k_sta == 0, other, mine)
    return jnp.concatenate([first, second], axis=0)[None]


def solution(mesh):
    in_specs = (
        P(),
        P(None, "gx"),
        P(),
        P("sta", "gy", None),
        P(None, "gx", "gy"),
        P(None, "gx", "gy"),
    )
    out_specs = P("sta", "gx", "gy", None)
    return jax.shard_map(
        on_device, mesh=mesh, in_specs=in_specs, out_specs=out_specs, check_vma=False
    )
```

```python
import math

import jax
import jax.numpy as jnp
from jax import lax
from jax.sharding import PartitionSpec as P

TIMES = 2
LINK_INV_Z = jnp.bfloat16
TAIL_CHUNKS = 2
GROUPS = 8
NOISE_POWER = 0.25
HIGHEST = lax.Precision.HIGHEST
DFT = lax.Precision.HIGH


def station_counts(station_group):
    labels = jnp.arange(GROUPS, dtype=jnp.int32)
    onehot = (station_group[:, None] == labels[None, :]).astype(jnp.float32)
    totals = jnp.sum(onehot, axis=0)
    return jnp.dot(onehot, totals, precision=HIGHEST)


def angles(rows, cols, length):
    product = rows[:, None] * cols[None, :] % length
    return product.astype(jnp.float32) * (2.0 * math.pi / length)


def local_coefficients(record, shifts, per_station):
    trace = record.shape[1]
    samples = jnp.arange(trace, dtype=jnp.int32)
    times = jnp.arange(TIMES, dtype=jnp.int32)
    positions = shifts[:, None, :] + times[None, :, None]
    hit = positions[:, :, :, None] == samples[None, None, None, :]
    values = jnp.sum(jnp.where(hit, record[:, None, None, :], 0.0), axis=3)
    scaled = values / per_station[:, None, None]
    return jnp.transpose(scaled, (1, 2, 0)).astype(jnp.bfloat16)


def complex_block(rows, cols, length, sign, scale):
    ang = angles(rows, cols, length)
    cos, sin = jnp.cos(ang) * scale, jnp.sin(ang) * scale
    if sign < 0:
        return jnp.stack([jnp.stack([cos, -sin], 1), jnp.stack([sin, cos], 1)], 0)
    return jnp.stack([jnp.stack([cos, sin], 1), jnp.stack([-sin, cos], 1)], 0)


def mirrored_psf(psf_real, psf_imag, k_sta, n_gx, n_gy, half, barrier=None):
    both = jnp.stack([psf_real, psf_imag])
    nz, bb, cb = both.shape[1], both.shape[2], both.shape[3]
    n = n_gx * n_gy

    def send(piece, di, dj):
        pairs = [(q * n + i * n_gy + j, (1 - q) * n + ((di - i) % n_gx) * n_gy + (dj - j) % n_gy)
                 for q in range(2) for i in range(n_gx) for j in range(n_gy)]
        return lax.ppermute(piece, ("sta", "gx", "gy"), pairs)

    rows = lax.dynamic_slice_in_dim(both, half - (half - 1) * (1 - k_sta), half, axis=2)
    main = send(rows, n_gx - 1, n_gy - 1)
    col = send(rows[:, :, :, :1], n_gx - 1, n_gy)
    row = send(both[:, :, :1], n_gx, n_gy - 1)
    corner = send(both[:, :, :1, :1], n_gx, n_gy)
    window = jnp.concatenate(
        [jnp.concatenate([main, col], axis=3), jnp.concatenate([row, corner], axis=3)], axis=2
    )
    ia = jnp.arange(nz, dtype=jnp.int32)
    flip_a = (ia[:, None] == (nz - ia[None, :]) % nz).astype(jnp.float32)
    it = jnp.arange(half + 1, dtype=jnp.int32)[:, None]
    tb = jnp.arange(half, dtype=jnp.int32)[None, :]
    flip_t = (it == half - 1 - tb + 1 - k_sta).astype(jnp.float32)
    iu = jnp.arange(cb + 1, dtype=jnp.int32)[:, None]
    uc = jnp.arange(cb, dtype=jnp.int32)[None, :]
    flip_u = (iu == cb - uc).astype(jnp.float32)
    window = lax.optimization_barrier(window) if barrier is None else lax.optimization_barrier((window, barrier))
    window, barrier = window if isinstance(window, tuple) else (window, None)
    out = jnp.einsum("rxyz,zc->rxyc", window, flip_u, precision=HIGHEST)
    out = jnp.einsum("rxyc,yb->rxbc", out, flip_t, precision=HIGHEST)
    return jnp.einsum("rxbc,xa->rabc", out, flip_a, precision=HIGHEST), barrier


def on_device(record, shifts, station_group, weights, psf_real, psf_imag):
    n_sta = lax.axis_size("sta")
    n_gx = lax.axis_size("gx")
    n_gy = lax.axis_size("gy")
    k_sta = lax.axis_index("sta")
    per_station = station_counts(station_group)
    own = weights.shape[0]
    depth = shifts.shape[1]
    rows = weights.shape[1]
    width = weights.shape[2]
    nz = depth * n_gx
    nx = rows * n_gy
    cb = width // n_gy
    bb = nx // n_gx
    zh = depth // n_sta
    bh = bb // n_sta
    n_grp = n_gx * n_sta
    pairs = [(i, (i + 1) % n_sta) for i in range(n_sta)]

    start = k_sta * own
    rec = lax.dynamic_slice_in_dim(record, start, own, 0)
    sh = lax.dynamic_slice_in_dim(shifts, start, own, 0)
    cnt = lax.dynamic_slice_in_dim(per_station, start, own, 0)
    coef = local_coefficients(rec, sh, cnt).reshape(TIMES * depth, own)
    partial = jnp.dot(
        coef, weights.reshape(own, rows * width), preferred_element_type=jnp.float32
    ).reshape(TIMES, depth, rows, width)
    keep = lax.dynamic_slice_in_dim(partial, k_sta * zh, zh, axis=1)
    send = lax.dynamic_slice_in_dim(partial, (1 - k_sta) * zh, zh, axis=1)
    field = keep + lax.ppermute(send, "sta", pairs)
    mirror, field = mirrored_psf(psf_real, psf_imag, k_sta, n_gx, n_gy, bh, field)

    iy = jnp.arange(width, dtype=jnp.int32)
    ix = jnp.arange(nx, dtype=jnp.int32)
    iz = jnp.arange(nz, dtype=jnp.int32)
    ty = complex_block(iy, iy, width, -1, 1.0).reshape(2, width, 2, n_gy, cb)
    s1 = jnp.einsum("szxy,syrjc->jrzxc", field, ty, precision=DFT)
    s1 = lax.all_to_all(s1, "gy", 0, 0, tiled=True)
    tx = complex_block(ix, ix, nx, -1, 1.0).reshape(2, n_gy, rows, 2, n_grp, bh)
    s2 = jnp.einsum("jszxc,sjxrLb->Lrbzc", s1, tx, precision=DFT)
    s2 = lax.all_to_all(s2, ("gx", "sta"), 0, 0, tiled=True)
    tz = complex_block(iz, iz, nz, -1, 1.0).reshape(2, n_grp, zh, 2, nz)
    s3 = jnp.einsum("Lsbzc,sLzra->rabc", s2, tz, precision=DFT)

    pr = lax.dynamic_slice_in_dim(psf_real, k_sta * bh, bh, axis=1)
    pi = lax.dynamic_slice_in_dim(psf_imag, k_sta * bh, bh, axis=1)
    pw = pr * pr + pi * pi + NOISE_POWER
    mr, mi = mirror[0], mirror[1]
    mw = mr * mr + mi * mi + NOISE_POWER
    we_re = 0.5 * (pr / pw + mr / mw)
    we_im = 0.5 * (mi / mw - pi / pw)
    h_re = we_re * s3[0] - we_im * s3[1]
    h_im = we_re * s3[1] + we_im * s3[0]
    filt = jnp.stack([h_re, h_im])

    tzi = complex_block(iz, iz, nz, 1, 1.0 / nz).reshape(2, nz, 2, n_grp, zh)
    g1 = jnp.einsum("sabc,sarLz->Lrzbc", filt, tzi, precision=DFT)
    if LINK_INV_Z is not None:
        g1 = g1.astype(LINK_INV_Z)
    txi = complex_block(ix, ix, nx, 1, 1.0 / nx).reshape(2, n_grp, bh, 2, n_gy, rows)
    tyi = complex_block(iy, iy, width, 1, 1.0 / width).reshape(2, n_gy, cb, 2, width)
    zt = zh // TAIL_CHUNKS
    mines, others = [], []
    for k in range(TAIL_CHUNKS):
        g1k = lax.all_to_all(g1[:, :, k * zt:(k + 1) * zt], ("gx", "sta"), 0, 0, tiled=True)
        g2 = jnp.einsum("Lszbc,sLbrjx->jrzxc", g1k.astype(jnp.float32), txi, precision=DFT)
        g2 = lax.all_to_all(g2, "gy", 0, 0, tiled=True)
        both = jnp.einsum("jszxc,sjcry->rzxy", g2, tyi, precision=DFT)
        mines.append(lax.dynamic_index_in_dim(both, k_sta, 0, keepdims=False))
        others.append(lax.ppermute(
            lax.dynamic_index_in_dim(both, 1 - k_sta, 0, keepdims=False), "sta", pairs))
    mine = jnp.concatenate(mines, axis=0)
    other = jnp.concatenate(others, axis=0)
    first = jnp.where(k_sta == 0, mine, other)
    second = jnp.where(k_sta == 0, other, mine)
    return jnp.concatenate([first, second], axis=0)[None]


def solution(mesh):
    in_specs = (
        P(),
        P(None, "gx"),
        P(),
        P("sta", "gy", None),
        P(None, "gx", "gy"),
        P(None, "gx", "gy"),
    )
    out_specs = P("sta", "gx", "gy", None)
    return jax.shard_map(
        on_device, mesh=mesh, in_specs=in_specs, out_specs=out_specs, check_vma=False
    )
```

```python
import math

import jax
import jax.numpy as jnp
from jax import lax
from jax.sharding import PartitionSpec as P

TIMES = 2
LINK_INV_Z = jnp.bfloat16
TAIL_CHUNKS = 2
GROUPS = 8
NOISE_POWER = 0.25
HIGHEST = lax.Precision.HIGHEST
DFT = lax.Precision.HIGH


def station_counts(station_group):
    labels = jnp.arange(GROUPS, dtype=jnp.int32)
    onehot = (station_group[:, None] == labels[None, :]).astype(jnp.float32)
    totals = jnp.sum(onehot, axis=0)
    return jnp.dot(onehot, totals, precision=HIGHEST)


def angles(rows, cols, length):
    product = rows[:, None] * cols[None, :] % length
    return product.astype(jnp.float32) * (2.0 * math.pi / length)


def local_coefficients(record, shifts, per_station):
    trace = record.shape[1]
    samples = jnp.arange(trace, dtype=jnp.int32)
    times = jnp.arange(TIMES, dtype=jnp.int32)
    positions = shifts[:, None, :] + times[None, :, None]
    hit = positions[:, :, :, None] == samples[None, None, None, :]
    values = jnp.sum(jnp.where(hit, record[:, None, None, :], 0.0), axis=3)
    scaled = values / per_station[:, None, None]
    return jnp.transpose(scaled, (1, 2, 0)).astype(jnp.bfloat16)


def complex_block(rows, cols, length, sign, scale):
    ang = angles(rows, cols, length)
    cos, sin = jnp.cos(ang) * scale, jnp.sin(ang) * scale
    if sign < 0:
        return jnp.stack([jnp.stack([cos, -sin], 1), jnp.stack([sin, cos], 1)], 0)
    return jnp.stack([jnp.stack([cos, sin], 1), jnp.stack([-sin, cos], 1)], 0)


def mirrored_psf(psf_real, psf_imag, k_sta, n_gx, n_gy, half, barrier=None):
    both = jnp.stack([psf_real, psf_imag])
    nz, bb, cb = both.shape[1], both.shape[2], both.shape[3]
    n = n_gx * n_gy

    def send(piece, di, dj):
        pairs = [(q * n + i * n_gy + j, (1 - q) * n + ((di - i) % n_gx) * n_gy + (dj - j) % n_gy)
                 for q in range(2) for i in range(n_gx) for j in range(n_gy)]
        return lax.ppermute(piece, ("sta", "gx", "gy"), pairs)

    rows = lax.dynamic_slice_in_dim(both, half - (half - 1) * (1 - k_sta), half, axis=2)
    main = send(rows, n_gx - 1, n_gy - 1)
    col = send(rows[:, :, :, :1], n_gx - 1, n_gy)
    row = send(both[:, :, :1], n_gx, n_gy - 1)
    corner = send(both[:, :, :1, :1], n_gx, n_gy)
    window = jnp.concatenate(
        [jnp.concatenate([main, col], axis=3), jnp.concatenate([row, corner], axis=3)], axis=2
    )
    ia = jnp.arange(nz, dtype=jnp.int32)
    flip_a = (ia[:, None] == (nz - ia[None, :]) % nz).astype(jnp.float32)
    it = jnp.arange(half + 1, dtype=jnp.int32)[:, None]
    tb = jnp.arange(half, dtype=jnp.int32)[None, :]
    flip_t = (it == half - 1 - tb + 1 - k_sta).astype(jnp.float32)
    iu = jnp.arange(cb + 1, dtype=jnp.int32)[:, None]
    uc = jnp.arange(cb, dtype=jnp.int32)[None, :]
    flip_u = (iu == cb - uc).astype(jnp.float32)
    window = lax.optimization_barrier(window) if barrier is None else lax.optimization_barrier((window, barrier))
    window, barrier = window if isinstance(window, tuple) else (window, None)
    out = jnp.einsum("rxyz,zc->rxyc", window, flip_u, precision=HIGHEST)
    out = jnp.einsum("rxyc,yb->rxbc", out, flip_t, precision=HIGHEST)
    return jnp.einsum("rxbc,xa->rabc", out, flip_a, precision=HIGHEST), barrier


def on_device(record, shifts, station_group, weights, psf_real, psf_imag):
    n_sta = lax.axis_size("sta")
    n_gx = lax.axis_size("gx")
    n_gy = lax.axis_size("gy")
    k_sta = lax.axis_index("sta")
    per_station = station_counts(station_group)
    own = weights.shape[0]
    depth = shifts.shape[1]
    rows = weights.shape[1]
    width = weights.shape[2]
    nz = depth * n_gx
    nx = rows * n_gy
    cb = width // n_gy
    bb = nx // n_gx
    zh = depth // n_sta
    bh = bb // n_sta
    n_grp = n_gx * n_sta
    pairs = [(i, (i + 1) % n_sta) for i in range(n_sta)]

    start = k_sta * own
    rec = lax.dynamic_slice_in_dim(record, start, own, 0)
    sh = lax.dynamic_slice_in_dim(shifts, start, own, 0)
    cnt = lax.dynamic_slice_in_dim(per_station, start, own, 0)
    coef = local_coefficients(rec, sh, cnt).reshape(TIMES * depth, own)
    partial = jnp.dot(
        coef, weights.reshape(own, rows * width), preferred_element_type=jnp.float32
    ).reshape(TIMES, depth, rows, width)
    keep = lax.dynamic_slice_in_dim(partial, k_sta * zh, zh, axis=1)
    send = lax.dynamic_slice_in_dim(partial, (1 - k_sta) * zh, zh, axis=1)
    field = keep + lax.ppermute(send, "sta", pairs)
    mirror, field = mirrored_psf(psf_real, psf_imag, k_sta, n_gx, n_gy, bh, field)

    iy = jnp.arange(width, dtype=jnp.int32)
    ix = jnp.arange(nx, dtype=jnp.int32)
    iz = jnp.arange(nz, dtype=jnp.int32)
    ty = complex_block(iy, iy, width, -1, 1.0).reshape(2, width, 2, n_gy, cb)
    s1 = jnp.einsum("szxy,syrjc->jrzxc", field, ty, precision=DFT)
    s1 = lax.all_to_all(s1, "gy", 0, 0, tiled=True)
    tx = complex_block(ix, ix, nx, -1, 1.0).reshape(2, n_gy, rows, 2, n_grp, bh)
    s2 = jnp.einsum("jszxc,sjxrLb->Lrbzc", s1, tx, precision=DFT)
    s2 = lax.all_to_all(s2, ("gx", "sta"), 0, 0, tiled=True)
    tz = complex_block(iz, iz, nz, -1, 1.0).reshape(2, n_grp, zh, 2, nz)
    s3 = jnp.einsum("Lsbzc,sLzra->rabc", s2, tz, precision=DFT)

    pr = lax.dynamic_slice_in_dim(psf_real, k_sta * bh, bh, axis=1)
    pi = lax.dynamic_slice_in_dim(psf_imag, k_sta * bh, bh, axis=1)
    pw = pr * pr + pi * pi + NOISE_POWER
    mr, mi = mirror[0], mirror[1]
    mw = mr * mr + mi * mi + NOISE_POWER
    we_re = 0.5 * (pr / pw + mr / mw)
    we_im = 0.5 * (mi / mw - pi / pw)
    h_re = we_re * s3[0] - we_im * s3[1]
    h_im = we_re * s3[1] + we_im * s3[0]
    filt = jnp.stack([h_re, h_im])

    tzi = complex_block(iz, iz, nz, 1, 1.0 / nz).reshape(2, nz, 2, n_grp, zh)
    g1 = jnp.einsum("sabc,sarLz->Lrzbc", filt, tzi, precision=DFT)
    if LINK_INV_Z is not None:
        g1 = g1.astype(LINK_INV_Z)
    g1 = lax.all_to_all(g1, ("gx", "sta"), 0, 0, tiled=True).astype(jnp.float32)
    txi = complex_block(ix, ix, nx, 1, 1.0 / nx).reshape(2, n_grp, bh, 2, n_gy, rows)
    tyi = complex_block(iy, iy, width, 1, 1.0 / width).reshape(2, n_gy, cb, 2, width)
    zt = zh // TAIL_CHUNKS
    mines, others = [], []
    for k in range(TAIL_CHUNKS):
        g2 = jnp.einsum("Lszbc,sLbrjx->jrzxc", g1[:, :, k * zt:(k + 1) * zt], txi, precision=DFT)
        g2 = lax.all_to_all(g2, "gy", 0, 0, tiled=True)
        t_other = lax.dynamic_index_in_dim(tyi, 1 - k_sta, 3, keepdims=False)
        others.append(lax.ppermute(
            jnp.einsum("jszxc,sjcy->zxy", g2, t_other, precision=DFT), "sta", pairs))
        t_mine = lax.dynamic_index_in_dim(tyi, k_sta, 3, keepdims=False)
        mines.append(jnp.einsum("jszxc,sjcy->zxy", g2, t_mine, precision=DFT))
    mine = jnp.concatenate(mines, axis=0)
    other = jnp.concatenate(others, axis=0)
    first = jnp.where(k_sta == 0, mine, other)
    second = jnp.where(k_sta == 0, other, mine)
    return jnp.concatenate([first, second], axis=0)[None]


def solution(mesh):
    in_specs = (
        P(),
        P(None, "gx"),
        P(),
        P("sta", "gy", None),
        P(None, "gx", "gy"),
        P(None, "gx", "gy"),
    )
    out_specs = P("sta", "gx", "gy", None)
    return jax.shard_map(
        on_device, mesh=mesh, in_specs=in_specs, out_specs=out_specs, check_vma=False
    )
```

```python
import math

import jax
import jax.numpy as jnp
from jax import lax
from jax.sharding import PartitionSpec as P

TIMES = 2
LINK_INV_Z = jnp.bfloat16
TAIL_CHUNKS = 2
GROUPS = 8
NOISE_POWER = 0.25
HIGHEST = lax.Precision.HIGHEST
DFT = lax.Precision.HIGH


def station_counts(station_group):
    labels = jnp.arange(GROUPS, dtype=jnp.int32)
    onehot = (station_group[:, None] == labels[None, :]).astype(jnp.float32)
    totals = jnp.sum(onehot, axis=0)
    return jnp.dot(onehot, totals, precision=HIGHEST)


def angles(rows, cols, length):
    product = rows[:, None] * cols[None, :] % length
    return product.astype(jnp.float32) * (2.0 * math.pi / length)


def local_coefficients(record, shifts, per_station):
    trace = record.shape[1]
    samples = jnp.arange(trace, dtype=jnp.int32)
    times = jnp.arange(TIMES, dtype=jnp.int32)
    positions = shifts[:, None, :] + times[None, :, None]
    hit = positions[:, :, :, None] == samples[None, None, None, :]
    values = jnp.sum(jnp.where(hit, record[:, None, None, :], 0.0), axis=3)
    scaled = values / per_station[:, None, None]
    return jnp.transpose(scaled, (1, 2, 0)).astype(jnp.bfloat16)


def complex_block(rows, cols, length, sign, scale):
    ang = angles(rows, cols, length)
    cos, sin = jnp.cos(ang) * scale, jnp.sin(ang) * scale
    if sign < 0:
        return jnp.stack([jnp.stack([cos, -sin], 1), jnp.stack([sin, cos], 1)], 0)
    return jnp.stack([jnp.stack([cos, sin], 1), jnp.stack([-sin, cos], 1)], 0)


def mirrored_psf(psf_real, psf_imag, k_sta, n_gx, n_gy, half, barrier=None):
    both = jnp.stack([psf_real, psf_imag])
    nz, bb, cb = both.shape[1], both.shape[2], both.shape[3]
    n = n_gx * n_gy

    def send(piece, di, dj):
        pairs = [(q * n + i * n_gy + j, (1 - q) * n + ((di - i) % n_gx) * n_gy + (dj - j) % n_gy)
                 for q in range(2) for i in range(n_gx) for j in range(n_gy)]
        return lax.ppermute(piece, ("sta", "gx", "gy"), pairs)

    rows = lax.dynamic_slice_in_dim(both, half - (half - 1) * (1 - k_sta), half, axis=2)
    main = send(rows, n_gx - 1, n_gy - 1)
    col = send(rows[:, :, :, :1], n_gx - 1, n_gy)
    row = send(both[:, :, :1], n_gx, n_gy - 1)
    corner = send(both[:, :, :1, :1], n_gx, n_gy)
    window = jnp.concatenate(
        [jnp.concatenate([main, col], axis=3), jnp.concatenate([row, corner], axis=3)], axis=2
    )
    ia = jnp.arange(nz, dtype=jnp.int32)
    flip_a = (ia[:, None] == (nz - ia[None, :]) % nz).astype(jnp.float32)
    it = jnp.arange(half + 1, dtype=jnp.int32)[:, None]
    tb = jnp.arange(half, dtype=jnp.int32)[None, :]
    flip_t = (it == half - 1 - tb + 1 - k_sta).astype(jnp.float32)
    iu = jnp.arange(cb + 1, dtype=jnp.int32)[:, None]
    uc = jnp.arange(cb, dtype=jnp.int32)[None, :]
    flip_u = (iu == cb - uc).astype(jnp.float32)
    window = lax.optimization_barrier(window) if barrier is None else lax.optimization_barrier((window, barrier))
    window, barrier = window if isinstance(window, tuple) else (window, None)
    out = jnp.einsum("rxyz,zc->rxyc", window, flip_u, precision=DFT)
    out = jnp.einsum("rxyc,yb->rxbc", out, flip_t, precision=DFT)
    return jnp.einsum("rxbc,xa->rabc", out, flip_a, precision=DFT), barrier


def on_device(record, shifts, station_group, weights, psf_real, psf_imag):
    n_sta = lax.axis_size("sta")
    n_gx = lax.axis_size("gx")
    n_gy = lax.axis_size("gy")
    k_sta = lax.axis_index("sta")
    per_station = station_counts(station_group)
    own = weights.shape[0]
    depth = shifts.shape[1]
    rows = weights.shape[1]
    width = weights.shape[2]
    nz = depth * n_gx
    nx = rows * n_gy
    cb = width // n_gy
    bb = nx // n_gx
    zh = depth // n_sta
    bh = bb // n_sta
    n_grp = n_gx * n_sta
    pairs = [(i, (i + 1) % n_sta) for i in range(n_sta)]

    start = k_sta * own
    rec = lax.dynamic_slice_in_dim(record, start, own, 0)
    sh = lax.dynamic_slice_in_dim(shifts, start, own, 0)
    cnt = lax.dynamic_slice_in_dim(per_station, start, own, 0)
    coef = local_coefficients(rec, sh, cnt).reshape(TIMES * depth, own)
    partial = jnp.dot(
        coef, weights.reshape(own, rows * width), preferred_element_type=jnp.float32
    ).reshape(TIMES, depth, rows, width)
    keep = lax.dynamic_slice_in_dim(partial, k_sta * zh, zh, axis=1)
    send = lax.dynamic_slice_in_dim(partial, (1 - k_sta) * zh, zh, axis=1)
    field = keep + lax.ppermute(send, "sta", pairs)
    mirror, field = mirrored_psf(psf_real, psf_imag, k_sta, n_gx, n_gy, bh, field)

    iy = jnp.arange(width, dtype=jnp.int32)
    ix = jnp.arange(nx, dtype=jnp.int32)
    iz = jnp.arange(nz, dtype=jnp.int32)
    ty = complex_block(iy, iy, width, -1, 1.0).reshape(2, width, 2, n_gy, cb)
    s1 = jnp.einsum("szxy,syrjc->jrzxc", field, ty, precision=DFT)
    s1 = lax.all_to_all(s1, "gy", 0, 0, tiled=True)
    tx = complex_block(ix, ix, nx, -1, 1.0).reshape(2, n_gy, rows, 2, n_grp, bh)
    s2 = jnp.einsum("jszxc,sjxrLb->Lrbzc", s1, tx, precision=DFT)
    s2 = lax.all_to_all(s2, ("gx", "sta"), 0, 0, tiled=True)
    tz = complex_block(iz, iz, nz, -1, 1.0).reshape(2, n_grp, zh, 2, nz)
    s3 = jnp.einsum("Lsbzc,sLzra->rabc", s2, tz, precision=DFT)

    pr = lax.dynamic_slice_in_dim(psf_real, k_sta * bh, bh, axis=1)
    pi = lax.dynamic_slice_in_dim(psf_imag, k_sta * bh, bh, axis=1)
    pw = pr * pr + pi * pi + NOISE_POWER
    mr, mi = mirror[0], mirror[1]
    mw = mr * mr + mi * mi + NOISE_POWER
    we_re = 0.5 * (pr / pw + mr / mw)
    we_im = 0.5 * (mi / mw - pi / pw)
    h_re = we_re * s3[0] - we_im * s3[1]
    h_im = we_re * s3[1] + we_im * s3[0]
    filt = jnp.stack([h_re, h_im])

    tzi = complex_block(iz, iz, nz, 1, 1.0 / nz).reshape(2, nz, 2, n_grp, zh)
    g1 = jnp.einsum("sabc,sarLz->Lrzbc", filt, tzi, precision=DFT)
    if LINK_INV_Z is not None:
        g1 = g1.astype(LINK_INV_Z)
    g1 = lax.all_to_all(g1, ("gx", "sta"), 0, 0, tiled=True).astype(jnp.float32)
    txi = complex_block(ix, ix, nx, 1, 1.0 / nx).reshape(2, n_grp, bh, 2, n_gy, rows)
    tyi = complex_block(iy, iy, width, 1, 1.0 / width).reshape(2, n_gy, cb, 2, width)
    zt = zh // TAIL_CHUNKS
    mines, others = [], []
    for k in range(TAIL_CHUNKS):
        g2 = jnp.einsum("Lszbc,sLbrjx->jrzxc", g1[:, :, k * zt:(k + 1) * zt], txi, precision=DFT)
        g2 = lax.all_to_all(g2, "gy", 0, 0, tiled=True)
        both = jnp.einsum("jszxc,sjcry->rzxy", g2, tyi, precision=DFT)
        mines.append(lax.dynamic_index_in_dim(both, k_sta, 0, keepdims=False))
        others.append(lax.ppermute(
            lax.dynamic_index_in_dim(both, 1 - k_sta, 0, keepdims=False), "sta", pairs))
    mine = jnp.concatenate(mines, axis=0)
    other = jnp.concatenate(others, axis=0)
    first = jnp.where(k_sta == 0, mine, other)
    second = jnp.where(k_sta == 0, other, mine)
    return jnp.concatenate([first, second], axis=0)[None]


def solution(mesh):
    in_specs = (
        P(),
        P(None, "gx"),
        P(),
        P("sta", "gy", None),
        P(None, "gx", "gy"),
        P(None, "gx", "gy"),
    )
    out_specs = P("sta", "gx", "gy", None)
    return jax.shard_map(
        on_device, mesh=mesh, in_specs=in_specs, out_specs=out_specs, check_vma=False
    )
```

```python
import math

import jax
import jax.numpy as jnp
from jax import lax
from jax.sharding import PartitionSpec as P

TIMES = 2
LINK_INV_Z = None
TAIL_CHUNKS = 2
GROUPS = 8
NOISE_POWER = 0.25
HIGHEST = lax.Precision.HIGHEST
DFT = lax.Precision.HIGH


def station_counts(station_group):
    labels = jnp.arange(GROUPS, dtype=jnp.int32)
    onehot = (station_group[:, None] == labels[None, :]).astype(jnp.float32)
    totals = jnp.sum(onehot, axis=0)
    return jnp.dot(onehot, totals, precision=HIGHEST)


def angles(rows, cols, length):
    product = rows[:, None] * cols[None, :] % length
    return product.astype(jnp.float32) * (2.0 * math.pi / length)


def local_coefficients(record, shifts, per_station):
    trace = record.shape[1]
    samples = jnp.arange(trace, dtype=jnp.int32)
    times = jnp.arange(TIMES, dtype=jnp.int32)
    positions = shifts[:, None, :] + times[None, :, None]
    hit = positions[:, :, :, None] == samples[None, None, None, :]
    values = jnp.sum(jnp.where(hit, record[:, None, None, :], 0.0), axis=3)
    scaled = values / per_station[:, None, None]
    return jnp.transpose(scaled, (1, 2, 0)).astype(jnp.bfloat16)


def complex_block(rows, cols, length, sign, scale):
    ang = angles(rows, cols, length)
    cos, sin = jnp.cos(ang) * scale, jnp.sin(ang) * scale
    if sign < 0:
        return jnp.stack([jnp.stack([cos, -sin], 1), jnp.stack([sin, cos], 1)], 0)
    return jnp.stack([jnp.stack([cos, sin], 1), jnp.stack([-sin, cos], 1)], 0)


def mirrored_psf(psf_real, psf_imag, k_sta, n_gx, n_gy, half, barrier=None):
    both = jnp.stack([psf_real, psf_imag])
    nz, bb, cb = both.shape[1], both.shape[2], both.shape[3]
    n = n_gx * n_gy

    def send(piece, di, dj):
        pairs = [(q * n + i * n_gy + j, (1 - q) * n + ((di - i) % n_gx) * n_gy + (dj - j) % n_gy)
                 for q in range(2) for i in range(n_gx) for j in range(n_gy)]
        return lax.ppermute(piece, ("sta", "gx", "gy"), pairs)

    rows = lax.dynamic_slice_in_dim(both, half - (half - 1) * (1 - k_sta), half, axis=2)
    main = send(rows, n_gx - 1, n_gy - 1)
    col = send(rows[:, :, :, :1], n_gx - 1, n_gy)
    row = send(both[:, :, :1], n_gx, n_gy - 1)
    corner = send(both[:, :, :1, :1], n_gx, n_gy)
    window = jnp.concatenate(
        [jnp.concatenate([main, col], axis=3), jnp.concatenate([row, corner], axis=3)], axis=2
    )
    ia = jnp.arange(nz, dtype=jnp.int32)
    flip_a = (ia[:, None] == (nz - ia[None, :]) % nz).astype(jnp.float32)
    it = jnp.arange(half + 1, dtype=jnp.int32)[:, None]
    tb = jnp.arange(half, dtype=jnp.int32)[None, :]
    flip_t = (it == half - 1 - tb + 1 - k_sta).astype(jnp.float32)
    iu = jnp.arange(cb + 1, dtype=jnp.int32)[:, None]
    uc = jnp.arange(cb, dtype=jnp.int32)[None, :]
    flip_u = (iu == cb - uc).astype(jnp.float32)
    window = lax.optimization_barrier(window) if barrier is None else lax.optimization_barrier((window, barrier))
    window, barrier = window if isinstance(window, tuple) else (window, None)
    out = jnp.einsum("rxyz,zc->rxyc", window, flip_u, precision=HIGHEST)
    out = jnp.einsum("rxyc,yb->rxbc", out, flip_t, precision=HIGHEST)
    return jnp.einsum("rxbc,xa->rabc", out, flip_a, precision=HIGHEST), barrier


def on_device(record, shifts, station_group, weights, psf_real, psf_imag):
    n_sta = lax.axis_size("sta")
    n_gx = lax.axis_size("gx")
    n_gy = lax.axis_size("gy")
    k_sta = lax.axis_index("sta")
    per_station = station_counts(station_group)
    own = weights.shape[0]
    depth = shifts.shape[1]
    rows = weights.shape[1]
    width = weights.shape[2]
    nz = depth * n_gx
    nx = rows * n_gy
    cb = width // n_gy
    bb = nx // n_gx
    zh = depth // n_sta
    bh = bb // n_sta
    n_grp = n_gx * n_sta
    pairs = [(i, (i + 1) % n_sta) for i in range(n_sta)]

    start = k_sta * own
    rec = lax.dynamic_slice_in_dim(record, start, own, 0)
    sh = lax.dynamic_slice_in_dim(shifts, start, own, 0)
    cnt = lax.dynamic_slice_in_dim(per_station, start, own, 0)
    coef = local_coefficients(rec, sh, cnt).reshape(TIMES * depth, own)
    partial = jnp.dot(
        coef, weights.reshape(own, rows * width), preferred_element_type=jnp.float32
    ).reshape(TIMES, depth, rows, width)
    keep = lax.dynamic_slice_in_dim(partial, k_sta * zh, zh, axis=1)
    send = lax.dynamic_slice_in_dim(partial, (1 - k_sta) * zh, zh, axis=1)
    field = keep + lax.ppermute(send, "sta", pairs)
    mirror, field = mirrored_psf(psf_real, psf_imag, k_sta, n_gx, n_gy, bh, field)

    iy = jnp.arange(width, dtype=jnp.int32)
    ix = jnp.arange(nx, dtype=jnp.int32)
    iz = jnp.arange(nz, dtype=jnp.int32)
    ty = complex_block(iy, iy, width, -1, 1.0).reshape(2, width, 2, n_gy, cb)
    s1 = jnp.einsum("szxy,syrjc->jrzxc", field, ty, precision=DFT)
    s1 = lax.all_to_all(s1, "gy", 0, 0, tiled=True)
    tx = complex_block(ix, ix, nx, -1, 1.0).reshape(2, n_gy, rows, 2, n_grp, bh)
    s2 = jnp.einsum("jszxc,sjxrLb->Lrbzc", s1, tx, precision=DFT)
    s2 = lax.all_to_all(s2.astype(jnp.bfloat16), ("gx", "sta"), 0, 0, tiled=True).astype(jnp.float32)
    tz = complex_block(iz, iz, nz, -1, 1.0).reshape(2, n_grp, zh, 2, nz)
    s3 = jnp.einsum("Lsbzc,sLzra->rabc", s2, tz, precision=DFT)

    pr = lax.dynamic_slice_in_dim(psf_real, k_sta * bh, bh, axis=1)
    pi = lax.dynamic_slice_in_dim(psf_imag, k_sta * bh, bh, axis=1)
    pw = pr * pr + pi * pi + NOISE_POWER
    mr, mi = mirror[0], mirror[1]
    mw = mr * mr + mi * mi + NOISE_POWER
    we_re = 0.5 * (pr / pw + mr / mw)
    we_im = 0.5 * (mi / mw - pi / pw)
    h_re = we_re * s3[0] - we_im * s3[1]
    h_im = we_re * s3[1] + we_im * s3[0]
    filt = jnp.stack([h_re, h_im])

    tzi = complex_block(iz, iz, nz, 1, 1.0 / nz).reshape(2, nz, 2, n_grp, zh)
    g1 = jnp.einsum("sabc,sarLz->Lrzbc", filt, tzi, precision=DFT)
    if LINK_INV_Z is not None:
        g1 = g1.astype(LINK_INV_Z)
    g1 = lax.all_to_all(g1, ("gx", "sta"), 0, 0, tiled=True).astype(jnp.float32)
    txi = complex_block(ix, ix, nx, 1, 1.0 / nx).reshape(2, n_grp, bh, 2, n_gy, rows)
    tyi = complex_block(iy, iy, width, 1, 1.0 / width).reshape(2, n_gy, cb, 2, width)
    zt = zh // TAIL_CHUNKS
    mines, others = [], []
    for k in range(TAIL_CHUNKS):
        g2 = jnp.einsum("Lszbc,sLbrjx->jrzxc", g1[:, :, k * zt:(k + 1) * zt], txi, precision=DFT)
        g2 = lax.all_to_all(g2, "gy", 0, 0, tiled=True)
        both = jnp.einsum("jszxc,sjcry->rzxy", g2, tyi, precision=DFT)
        mines.append(lax.dynamic_index_in_dim(both, k_sta, 0, keepdims=False))
        others.append(lax.ppermute(
            lax.dynamic_index_in_dim(both, 1 - k_sta, 0, keepdims=False), "sta", pairs))
    mine = jnp.concatenate(mines, axis=0)
    other = jnp.concatenate(others, axis=0)
    first = jnp.where(k_sta == 0, mine, other)
    second = jnp.where(k_sta == 0, other, mine)
    return jnp.concatenate([first, second], axis=0)[None]


def solution(mesh):
    in_specs = (
        P(),
        P(None, "gx"),
        P(),
        P("sta", "gy", None),
        P(None, "gx", "gy"),
        P(None, "gx", "gy"),
    )
    out_specs = P("sta", "gx", "gy", None)
    return jax.shard_map(
        on_device, mesh=mesh, in_specs=in_specs, out_specs=out_specs, check_vma=False
    )
```
